128 devices in a mesh: space: 8 (over z_hi, x), blk: 16 (over y, z_lo, core).
Axes of the slice: x: 4, y: 4, z: 4 (z_hi: 2, z_lo: 2; z = z_hi * 2 + z_lo), core: 2. Of those that a mesh axis runs over, the one named last changes fastest.
Arguments:
- density: bfloat16 [12288, 128, 128], P(('space', 'blk')), may hold values from -6 to 6
- bra_table: bfloat16 [12288, 128, 256], P(('space', 'blk')), may hold values from -0.5 to 0.5
- ket_table: bfloat16 [12288, 128, 256], P(('space', 'blk')), may hold values from -0.5 to 0.5
- box_of_block: int32 [12288], P(('space', 'blk')), may hold values from 0 to 127
- leaf_src: int32 [1024, 27], P(('space', 'blk')), may hold values from 0 to 383
- leaf_type: int32 [1024, 27], P(('space', 'blk')), may hold values from 0 to 15
- coarse_src: int32 [128, 27], P(('space', 'blk')), may hold values from 0 to 127
- coarse_type: int32 [128, 27], P(('space', 'blk')), may hold values from 0 to 15
- translation: float32 [16, 256, 256], replicated, may hold values from -0.375 to 0.375
- upward_translation_table: float32 [8, 256, 256], replicated, may hold values from -0.375 to 0.375
Outputs:
- coulomb: bfloat16 [12288, 128, 128], P(('space', 'blk'))
- box_locals: float32 [1024, 256], P(('space', 'blk'))
The draws below stay inside these ranges and needn't reach their ends.
All inputs are finite; a program needn't handle non-finite values.
Results may differ from the reference program's by a relative error of at most 0.0049.
Values sent between devices are 32-bit elements; how exact they have to be, the bound alone decides.
No kernel may reach another device: no remote copies, remote signals or barrier semaphores. Data moves between devices by JAX's collectives and lax.ppermute only.
A program may use at most 128 MiB of HBM per device.

```python
import math
import jax
import jax.numpy as jnp
import numpy as np
from jax import lax

BS = 128
COEFF_COUNT = 256
BLK_DEV = 96
NLIST = 27
NCOARSE = 27
NTYPE = 16
BOX_DOM = 128
LEAF_BOX_COUNT = 1024
PARENTS = 128
BLOCKS = 12288
N_SPACE = 8
N_BLK = 16


def place_ends(drawn, own_key, low, high):
    longest = drawn.shape.index(max(drawn.shape))
    spots = []
    for shift in (0, 1):
        where = [jax.random.randint(jax.random.fold_in(own_key, axis), (), 0, length) for axis, length in enumerate(drawn.shape)]
        where[longest] = (where[longest] + shift) % drawn.shape[longest]
        spots.append(tuple(where))
    return drawn.at[spots[0]].set(low).at[spots[1]].set(high)


def shard_levels(key, shape, shards, low, high):
    gain = 1.0
    for position, parts in shards:
        heights = jax.random.uniform(jax.random.fold_in(jax.random.fold_in(key, 6), position), (parts,), jnp.float32, low / len(shards), high / len(shards))
        gain = gain * jnp.repeat(jnp.exp(heights), shape[position] // parts).reshape((-1,) + (1,) * (len(shape) - 1 - position))
    return gain


def rank_table(number_of, slope):
    loads = [(1 << 20) // math.isqrt(rank ** slope) + 1 for rank in range(1, number_of + 1)]
    scale = 1 + sum(loads) // (1 << 30)
    return np.cumsum(np.array([max(1, weight // scale) for weight in loads]))


def ranked(rng, shape, count, slope):
    grid = rank_table(count, slope)
    pick = jax.random.randint(jax.random.fold_in(rng, 1), shape, 0, int(grid[count - 1]))
    grade = jnp.searchsorted(jnp.asarray(grid, jnp.int32), pick, side="right")
    return jax.random.permutation(jax.random.fold_in(rng, 2), count)[grade].astype(jnp.int32)


def gaussian(key, dims, deviation, most, pieces=(), held_as=jnp.bfloat16):
    loudness = shard_levels(key, dims, pieces, -0.22, 0.18) if pieces else 1.0
    entries = jax.random.normal(key, dims, jnp.float32) * deviation * loudness
    return jnp.minimum(jnp.maximum(entries, -most), most).astype(held_as)


def setup_inputs(seed: int = 0) -> dict:
    seeds = jax.random.split(jax.random.key(seed), 11)
    return {
        "density": gaussian(seeds[0], (BLOCKS, BS, BS), 1.0, 6.0, ((0, 128),)),
        "bra_table": gaussian(seeds[1], (BLOCKS, BS, COEFF_COUNT), BS ** -0.5, 0.5, ((0, 128),)),
        "ket_table": gaussian(seeds[2], (BLOCKS, BS, COEFF_COUNT), BS ** -0.5, 0.5, ((0, 128),)),
        "box_of_block": place_ends(ranked(seeds[3], (BLOCKS,), BOX_DOM, 2), jax.random.fold_in(seeds[3], 3), 0, BOX_DOM - 1).astype(jnp.int32),
        "leaf_src": place_ends(jax.random.randint(seeds[4], (LEAF_BOX_COUNT, NLIST), 0, 3 * BOX_DOM), jax.random.fold_in(seeds[4], 1), 0, (3 * BOX_DOM) - 1).astype(jnp.int32),
        "leaf_type": place_ends(jax.random.randint(seeds[5], (LEAF_BOX_COUNT, NLIST), 0, NTYPE), jax.random.fold_in(seeds[5], 1), 0, NTYPE - 1).astype(jnp.int32),
        "coarse_src": place_ends(jax.random.randint(seeds[6], (PARENTS, NCOARSE), 0, PARENTS), jax.random.fold_in(seeds[6], 1), 0, PARENTS - 1).astype(jnp.int32),
        "coarse_type": place_ends(jax.random.randint(seeds[7], (PARENTS, NCOARSE), 0, NTYPE), jax.random.fold_in(seeds[7], 1), 0, NTYPE - 1).astype(jnp.int32),
        "translation": gaussian(seeds[8], (NTYPE, COEFF_COUNT, COEFF_COUNT), COEFF_COUNT ** -0.5, 0.375, (), jnp.float32),
        "upward_translation_table": gaussian(seeds[9], (8, COEFF_COUNT, COEFF_COUNT), COEFF_COUNT ** -0.5, 0.375, (), jnp.float32),
    }


def block_group_moments(group):
    dens, bra, ket = group
    inner = jnp.einsum('bmn,bmk->bnk', dens.astype(jnp.float32), bra.astype(jnp.float32), precision=lax.Precision.HIGHEST)
    return jnp.sum(inner * ket.astype(jnp.float32), axis=1)


def reference(density, bra_table, ket_table, box_of_block, leaf_src, leaf_type, coarse_src, coarse_type, translation, upward_translation_table):
    top_level_index = lax.Precision.HIGHEST
    groups = N_SPACE * N_BLK
    dens_g = density.reshape(groups, BLK_DEV, BS, BS)
    bra_g = bra_table.reshape(groups, BLK_DEV, BS, COEFF_COUNT)
    ket_g = ket_table.reshape(groups, BLK_DEV, BS, COEFF_COUNT)
    moments = lax.map(block_group_moments, (dens_g, bra_g, ket_g)).reshape(N_SPACE, N_BLK * BLK_DEV, COEFF_COUNT)
    boxes = box_of_block.reshape(N_SPACE, N_BLK * BLK_DEV)
    box_hot = (boxes[:, :, None] == jnp.arange(BOX_DOM, dtype=jnp.int32)[None, None, :]).astype(jnp.float32)
    leaf_moments = jnp.einsum('sbj,sbk->sjk', box_hot, moments, precision=top_level_index)
    padded = jnp.concatenate([jnp.zeros((1, BOX_DOM, COEFF_COUNT), jnp.float32), leaf_moments, jnp.zeros((1, BOX_DOM, COEFF_COUNT), jnp.float32)], axis=0)
    windows = jnp.stack([padded[s:s + 3].reshape(3 * BOX_DOM, COEFF_COUNT) for s in range(N_SPACE)])
    src_hot = (leaf_src.reshape(N_SPACE, BOX_DOM, NLIST)[..., None] == jnp.arange(3 * BOX_DOM, dtype=jnp.int32)).astype(jnp.float32)
    type_hot = (leaf_type.reshape(N_SPACE, BOX_DOM, NLIST)[..., None] == jnp.arange(NTYPE, dtype=jnp.int32)).astype(jnp.float32)
    counts = jnp.einsum('sblt,sblj->sbtj', type_hot, src_hot, precision=top_level_index)
    gathered = jnp.einsum('sbtj,sjk->sbtk', counts, windows, precision=top_level_index)
    leaf_far = jnp.einsum('sbtk,tlk->sbl', gathered, translation, precision=top_level_index).reshape(LEAF_BOX_COUNT, COEFF_COUNT)
    child_boxes = leaf_moments.reshape(PARENTS, 8, COEFF_COUNT)
    parent_multipole_rows = jnp.einsum('ins,nrs->ir', child_boxes, upward_translation_table, precision=top_level_index)
    csrc_hot = (coarse_src[..., None] == jnp.arange(PARENTS, dtype=jnp.int32)).astype(jnp.float32)
    ctype_hot = (coarse_type[..., None] == jnp.arange(NTYPE, dtype=jnp.int32)).astype(jnp.float32)
    ccounts = jnp.einsum('pet,peq->ptq', ctype_hot, csrc_hot, precision=top_level_index)
    cgathered = jnp.einsum('ptq,qk->ptk', ccounts, parent_multipole_rows, precision=top_level_index)
    parent_local_rows = jnp.einsum('ptk,tlk->pl', cgathered, translation, precision=top_level_index)
    downward_sent = jnp.einsum('uh,nhq->unq', parent_local_rows, upward_translation_table, precision=top_level_index).reshape(LEAF_BOX_COUNT, COEFF_COUNT)
    box_locals = leaf_far + downward_sent
    dom_locals = box_locals.reshape(N_SPACE, BOX_DOM, COEFF_COUNT)
    block_locals = jnp.einsum('sbj,sjk->sbk', box_hot, dom_locals, precision=top_level_index).reshape(groups, BLK_DEV, COEFF_COUNT)

    def contract(group):
        bra, ket, local = group
        scaled = (bra.astype(jnp.float32) * local[:, None, :]).astype(jnp.bfloat16)
        return jnp.einsum('bmk,bnk->bmn', scaled.astype(jnp.float32), ket.astype(jnp.float32), precision=top_level_index).astype(jnp.bfloat16)

    coulomb = lax.map(contract, (bra_g, ket_g, block_locals)).reshape(BLOCKS, BS, BS)
    return coulomb, box_locals
```

```python
import jax
import jax.numpy as jnp
from jax import lax
from jax.sharding import PartitionSpec as P


def exchange(x, axis, mask):
    count = lax.axis_size(axis)
    return lax.ppermute(x, axis, [(i, i ^ mask) for i in range(count)])


def butterfly_sum(x, axis):
    count = lax.axis_size(axis)
    mask = 1
    while mask < count:
        x = x + exchange(x, axis, mask)
        mask *= 2
    return x


def butterfly_gather(x, axis):
    count = lax.axis_size(axis)
    me = lax.axis_index(axis)
    mask = 1
    while mask < count:
        other = exchange(x, axis, mask)
        low = (me // mask) % 2 == 0
        x = jnp.where(low, jnp.concatenate([x, other], 0), jnp.concatenate([other, x], 0))
        mask *= 2
    return x


def neighbours(block, axis):
    count = lax.axis_size(axis)
    forward = [(i, i + 1) for i in range(count - 1)]
    backward = [(target, source) for source, target in forward]
    low = lax.ppermute(block, axis, forward)
    high = lax.ppermute(block, axis, backward)
    return jnp.concatenate([low, block, high], axis=0)


def shards(
    density,
    bra_table,
    ket_table,
    box_of_block,
    leaf_src,
    leaf_type,
    coarse_src,
    coarse_type,
    translation,
    upward_translation_table,
):
    top = lax.Precision.HIGHEST
    n_blk = lax.axis_size("blk")
    box_dom = 8 * n_blk
    n_types = translation.shape[0]
    inner = jnp.einsum("bmn,bmk->bnk", density, bra_table, preferred_element_type=jnp.float32)
    moments = jnp.sum(inner * ket_table.astype(jnp.float32), axis=1)
    box_hot = (box_of_block[:, None] == jnp.arange(box_dom, dtype=jnp.int32)[None, :]).astype(
        jnp.float32
    )
    partial_moments = lax.dot_general(
        box_hot, moments, (((0,), (0,)), ((), ())), precision=top
    )
    domain = butterfly_sum(partial_moments, "blk")
    window = neighbours(domain, "space")
    domain_parents = jnp.einsum(
        "qce,cde->qd", domain.reshape(n_blk, 8, -1), upward_translation_table, precision=top
    )
    all_parents = butterfly_gather(domain_parents, "space")
    src_hot = (leaf_src[..., None] == jnp.arange(3 * box_dom, dtype=jnp.int32)).astype(jnp.float32)
    type_hot = (leaf_type[..., None] == jnp.arange(n_types, dtype=jnp.int32)).astype(jnp.float32)
    counts = jnp.einsum("blt,blj->btj", type_hot, src_hot, precision=top)
    gathered = jnp.einsum("btj,jk->btk", counts, window, precision=top)
    leaf_far = jnp.einsum("btk,tlk->bl", gathered, translation, precision=top)
    n_parents = all_parents.shape[0]
    csrc_hot = (coarse_src[..., None] == jnp.arange(n_parents, dtype=jnp.int32)).astype(jnp.float32)
    ctype_hot = (coarse_type[..., None] == jnp.arange(n_types, dtype=jnp.int32)).astype(jnp.float32)
    ccounts = jnp.einsum("pet,peq->ptq", ctype_hot, csrc_hot, precision=top)
    cgathered = jnp.einsum("ptq,qk->ptk", ccounts, all_parents, precision=top)
    parent_local_expansion = jnp.einsum("ptk,tlk->pl", cgathered, translation, precision=top)
    downward_sent = jnp.einsum(
        "d,uds->us", parent_local_expansion[0], upward_translation_table, precision=top
    )
    box_locals = leaf_far + downward_sent
    domain_local = butterfly_gather(box_locals, "blk")
    block_locals = jnp.dot(box_hot, domain_local, precision=top)
    scaled = (bra_table.astype(jnp.float32) * block_locals[:, None, :]).astype(jnp.bfloat16)
    coulomb = jnp.einsum(
        "bmk,bnk->bmn", scaled, ket_table, preferred_element_type=jnp.float32
    ).astype(jnp.bfloat16)
    return (coulomb, box_locals)


def solution(mesh):
    placed = (
        P(("space", "blk"), None, None),
        P(("space", "blk"), None, None),
        P(("space", "blk"), None, None),
        P(("space", "blk")),
        P(("space", "blk"), None),
        P(("space", "blk"), None),
        P(("space", "blk"), None),
        P(("space", "blk"), None),
        P(),
        P(),
    )
    return jax.shard_map(
        shards,
        mesh=mesh,
        in_specs=placed,
        out_specs=(P(("space", "blk"), None, None), P(("space", "blk"), None)),
        check_vma=False,
    )
```

```python
import jax
import jax.numpy as jnp
from jax import lax
from jax.sharding import PartitionSpec as P


def exchange(x, axis, mask):
    count = lax.axis_size(axis)
    return lax.ppermute(x, axis, [(i, i ^ mask) for i in range(count)])


def shift(x, axis, step):
    count = lax.axis_size(axis)
    return lax.ppermute(x, axis, [(i, (i + step) % count) for i in range(count)])


def group_sum(x, axis):
    count = lax.axis_size(axis)
    stride = 1
    while stride < count:
        if count % (4 * stride) == 0:
            near = x + exchange(x, axis, stride)
            far = exchange(x, axis, 2 * stride) + exchange(x, axis, 3 * stride)
            x = near + far
            stride *= 4
        else:
            x = x + exchange(x, axis, stride)
            stride *= 2
    return x


def shards(
    density,
    bra_table,
    ket_table,
    box_of_block,
    leaf_src,
    leaf_type,
    coarse_src,
    coarse_type,
    translation,
    upward_translation_table,
):
    top = lax.Precision.HIGHEST
    n_blk = lax.axis_size("blk")
    n_space = lax.axis_size("space")
    me = lax.axis_index("blk")
    here = lax.axis_index("space")
    leaves = leaf_src.shape[0]
    box_dom = leaves * n_blk
    n_types = translation.shape[0]
    coeffs = translation.shape[1]

    lists = jnp.concatenate([leaf_src, leaf_type, coarse_src, coarse_type], axis=0)
    table = jnp.zeros((n_blk,) + lists.shape, jnp.int32)
    table = lax.dynamic_update_index_in_dim(table, lists, me, 0)
    table = group_sum(table, "blk")
    dom_src = table[:, :leaves].reshape(box_dom, -1)
    dom_type = table[:, leaves : 2 * leaves].reshape(box_dom, -1)
    dom_csrc = table[:, 2 * leaves]
    dom_ctype = table[:, 2 * leaves + 1]

    inner = jnp.einsum("bmn,bmk->bnk", density, bra_table, preferred_element_type=jnp.float32)
    moments = jnp.sum(inner * ket_table.astype(jnp.float32), axis=1)
    box_hot = (box_of_block[:, None] == jnp.arange(box_dom, dtype=jnp.int32)[None, :]).astype(
        jnp.float32
    )
    partial_moments = lax.dot_general(
        box_hot, moments, (((0,), (0,)), ((), ())), precision=top
    )
    domain = group_sum(partial_moments, "blk")
    domain_parents = jnp.einsum(
        "qce,cde->qd", domain.reshape(n_blk, leaves, coeffs), upward_translation_table, precision=top
    )
    near = jnp.concatenate([domain, domain_parents], axis=0)
    from_low = shift(near, "space", 1)
    from_high = shift(near, "space", n_space - 1)
    low = jnp.where(here > 0, from_low[:box_dom], 0.0)
    high = jnp.where(here < n_space - 1, from_high[:box_dom], 0.0)
    window = jnp.concatenate([low, domain, high], axis=0)
    by_step = [domain_parents, from_low[box_dom:]]
    by_step += [shift(domain_parents, "space", k) for k in range(2, n_space - 1)]
    by_step += [from_high[box_dom:]]
    all_parents = jnp.concatenate(by_step, axis=0)
    csrc = ((here - dom_csrc // n_blk) % n_space) * n_blk + dom_csrc % n_blk

    src_hot = (dom_src[..., None] == jnp.arange(3 * box_dom, dtype=jnp.int32)).astype(jnp.bfloat16)
    type_hot = (dom_type[..., None] == jnp.arange(n_types, dtype=jnp.int32)).astype(jnp.bfloat16)
    counts = jnp.einsum("blt,blj->btj", type_hot, src_hot, preferred_element_type=jnp.float32)
    gathered = jnp.einsum("btj,jk->btk", counts, window, precision=top)
    n_parents = all_parents.shape[0]
    csrc_hot = (csrc[..., None] == jnp.arange(n_parents, dtype=jnp.int32)).astype(jnp.bfloat16)
    ctype_hot = (dom_ctype[..., None] == jnp.arange(n_types, dtype=jnp.int32)).astype(jnp.bfloat16)
    ccounts = jnp.einsum("pet,peq->ptq", ctype_hot, csrc_hot, preferred_element_type=jnp.float32)
    cgathered = jnp.einsum("ptq,qk->ptk", ccounts, all_parents, precision=top)
    rows = jnp.concatenate([gathered, cgathered], axis=0)
    far = jnp.einsum("btk,tlk->bl", rows, translation, precision=top)
    leaf_far = far[:box_dom]
    parent_locals = far[box_dom:]
    downward = jnp.einsum(
        "qd,cds->qcs", parent_locals, upward_translation_table, precision=top
    ).reshape(box_dom, coeffs)
    domain_local = leaf_far + downward
    box_locals = lax.dynamic_slice_in_dim(domain_local, me * leaves, leaves, axis=0)
    block_locals = jnp.dot(box_hot, domain_local, precision=top)
    scaled = (bra_table.astype(jnp.float32) * block_locals[:, None, :]).astype(jnp.bfloat16)
    coulomb = jnp.einsum(
        "bmk,bnk->bmn", scaled, ket_table, preferred_element_type=jnp.float32
    ).astype(jnp.bfloat16)
    return (coulomb, box_locals)


def solution(mesh):
    placed = (
        P(("space", "blk"), None, None),
        P(("space", "blk"), None, None),
        P(("space", "blk"), None, None),
        P(("space", "blk")),
        P(("space", "blk"), None),
        P(("space", "blk"), None),
        P(("space", "blk"), None),
        P(("space", "blk"), None),
        P(),
        P(),
    )
    return jax.shard_map(
        shards,
        mesh=mesh,
        in_specs=placed,
        out_specs=(P(("space", "blk"), None, None), P(("space", "blk"), None)),
        check_vma=False,
    )
```

```python
import jax
import jax.numpy as jnp
from jax import lax
from jax.sharding import PartitionSpec as P


def exchange(x, axis, mask):
    count = lax.axis_size(axis)
    return lax.ppermute(x, axis, [(i, i ^ mask) for i in range(count)])


def butterfly_sum(x, axis):
    count = lax.axis_size(axis)
    mask = 1
    while mask < count:
        x = x + exchange(x, axis, mask)
        mask *= 2
    return x


def butterfly_gather(x, axis):
    count = lax.axis_size(axis)
    me = lax.axis_index(axis)
    mask = 1
    while mask < count:
        other = exchange(x, axis, mask)
        low = (me // mask) % 2 == 0
        x = jnp.where(low, jnp.concatenate([x, other], 0), jnp.concatenate([other, x], 0))
        mask *= 2
    return x


def shards(
    density,
    bra_table,
    ket_table,
    box_of_block,
    leaf_src,
    leaf_type,
    coarse_src,
    coarse_type,
    translation,
    upward_translation_table,
):
    top = lax.Precision.HIGHEST
    n_blk = lax.axis_size("blk")
    n_space = lax.axis_size("space")
    me = lax.axis_index("blk")
    here = lax.axis_index("space")
    leaves = leaf_src.shape[0]
    box_dom = leaves * n_blk
    n_types = translation.shape[0]
    coeffs = translation.shape[1]

    lists = jnp.concatenate([leaf_src, leaf_type, coarse_src, coarse_type], axis=0)
    flat = lists.size
    table = jnp.zeros((n_blk, flat), jnp.float32)
    table = lax.dynamic_update_index_in_dim(table, lists.reshape(flat).astype(jnp.float32), me, 0)
    table_rows = -(-n_blk * flat // coeffs)
    table = jnp.pad(table.reshape(-1), (0, table_rows * coeffs - n_blk * flat))
    table = table.reshape(table_rows, coeffs)

    inner = jnp.einsum("bmn,bmk->bnk", density, bra_table, preferred_element_type=jnp.float32)
    moments = jnp.sum(inner * ket_table.astype(jnp.float32), axis=1)
    box_hot = (box_of_block[:, None] == jnp.arange(box_dom, dtype=jnp.int32)[None, :]).astype(
        jnp.float32
    )
    partial_moments = lax.dot_general(
        box_hot, moments, (((0,), (0,)), ((), ())), precision=top
    )
    summed = butterfly_sum(jnp.concatenate([partial_moments, table], axis=0), "blk")
    domain = summed[:box_dom]
    table = summed[box_dom:].reshape(-1)[: n_blk * flat].reshape((n_blk,) + lists.shape)
    table = table.astype(jnp.int32)
    dom_src = table[:, :leaves].reshape(box_dom, -1)
    dom_type = table[:, leaves : 2 * leaves].reshape(box_dom, -1)
    dom_csrc = table[:, 2 * leaves]
    dom_ctype = table[:, 2 * leaves + 1]

    domain_parents = jnp.einsum(
        "qce,cde->qd", domain.reshape(n_blk, leaves, coeffs), upward_translation_table, precision=top
    )
    everything = butterfly_gather(
        jnp.concatenate([domain, domain_parents], axis=0)[None], "space"
    )
    all_leaves = everything[:, :box_dom]
    all_parents = everything[:, box_dom:].reshape(-1, coeffs)
    zero = jnp.zeros((1, box_dom, coeffs), jnp.float32)
    padded = jnp.concatenate([zero, all_leaves, zero], axis=0)
    window = lax.dynamic_slice_in_dim(padded, here, 3, axis=0).reshape(3 * box_dom, coeffs)

    src_hot = (dom_src[..., None] == jnp.arange(3 * box_dom, dtype=jnp.int32)).astype(jnp.bfloat16)
    type_hot = (dom_type[..., None] == jnp.arange(n_types, dtype=jnp.int32)).astype(jnp.bfloat16)
    counts = jnp.einsum("blt,blj->btj", type_hot, src_hot, preferred_element_type=jnp.float32)
    gathered = jnp.einsum("btj,jk->btk", counts, window, precision=top)
    n_parents = all_parents.shape[0]
    csrc_hot = (dom_csrc[..., None] == jnp.arange(n_parents, dtype=jnp.int32)).astype(jnp.bfloat16)
    ctype_hot = (dom_ctype[..., None] == jnp.arange(n_types, dtype=jnp.int32)).astype(jnp.bfloat16)
    ccounts = jnp.einsum("pet,peq->ptq", ctype_hot, csrc_hot, preferred_element_type=jnp.float32)
    cgathered = jnp.einsum("ptq,qk->ptk", ccounts, all_parents, precision=top)
    rows = jnp.concatenate([gathered, cgathered], axis=0)
    far = jnp.einsum("btk,tlk->bl", rows, translation, precision=top)
    leaf_far = far[:box_dom]
    parent_locals = far[box_dom:]
    downward = jnp.einsum(
        "qd,cds->qcs", parent_locals, upward_translation_table, precision=top
    ).reshape(box_dom, coeffs)
    domain_local = leaf_far + downward
    box_locals = lax.dynamic_slice_in_dim(domain_local, me * leaves, leaves, axis=0)
    block_locals = jnp.dot(box_hot, domain_local, precision=top)
    scaled = (bra_table.astype(jnp.float32) * block_locals[:, None, :]).astype(jnp.bfloat16)
    coulomb = jnp.einsum(
        "bmk,bnk->bmn", scaled, ket_table, preferred_element_type=jnp.float32
    ).astype(jnp.bfloat16)
    return (coulomb, box_locals)


def solution(mesh):
    placed = (
        P(("space", "blk"), None, None),
        P(("space", "blk"), None, None),
        P(("space", "blk"), None, None),
        P(("space", "blk")),
        P(("space", "blk"), None),
        P(("space", "blk"), None),
        P(("space", "blk"), None),
        P(("space", "blk"), None),
        P(),
        P(),
    )
    return jax.shard_map(
        shards,
        mesh=mesh,
        in_specs=placed,
        out_specs=(P(("space", "blk"), None, None), P(("space", "blk"), None)),
        check_vma=False,
    )
```

```python
import jax
import jax.numpy as jnp
from jax import lax
from jax.sharding import PartitionSpec as P


def exchange(x, axis, mask):
    count = lax.axis_size(axis)
    return lax.ppermute(x, axis, [(i, i ^ mask) for i in range(count)])


def butterfly_sum(x, axis):
    count = lax.axis_size(axis)
    mask = 1
    while mask < count:
        x = x + exchange(x, axis, mask)
        mask *= 2
    return x


def butterfly_gather(x, axis):
    count = lax.axis_size(axis)
    me = lax.axis_index(axis)
    mask = 1
    while mask < count:
        other = exchange(x, axis, mask)
        low = (me // mask) % 2 == 0
        x = jnp.where(low, jnp.concatenate([x, other], 0), jnp.concatenate([other, x], 0))
        mask *= 2
    return x


def shards(
    density,
    bra_table,
    ket_table,
    box_of_block,
    leaf_src,
    leaf_type,
    coarse_src,
    coarse_type,
    translation,
    upward_translation_table,
):
    top = lax.Precision.HIGH
    n_blk = lax.axis_size("blk")
    n_space = lax.axis_size("space")
    me = lax.axis_index("blk")
    here = lax.axis_index("space")
    leaves = leaf_src.shape[0]
    box_dom = leaves * n_blk
    n_types = translation.shape[0]
    coeffs = translation.shape[1]

    lists = jnp.concatenate([leaf_src, leaf_type, coarse_src, coarse_type], axis=0)
    flat = lists.size
    table = jnp.zeros((n_blk, flat), jnp.float32)
    table = lax.dynamic_update_index_in_dim(table, lists.reshape(flat).astype(jnp.float32), me, 0)
    table_rows = -(-n_blk * flat // coeffs)
    table = jnp.pad(table.reshape(-1), (0, table_rows * coeffs - n_blk * flat))
    table = table.reshape(table_rows, coeffs)

    inner = jnp.einsum("bmn,bmk->bnk", density, bra_table, preferred_element_type=jnp.float32)
    moments = jnp.sum(inner * ket_table.astype(jnp.float32), axis=1)
    box_hot = (box_of_block[:, None] == jnp.arange(box_dom, dtype=jnp.int32)[None, :]).astype(
        jnp.float32
    )
    partial_moments = lax.dot_general(
        box_hot, moments, (((0,), (0,)), ((), ())), precision=top
    )
    summed = butterfly_sum(jnp.concatenate([partial_moments, table], axis=0), "blk")
    domain = summed[:box_dom]
    table = summed[box_dom:].reshape(-1)[: n_blk * flat].reshape((n_blk,) + lists.shape)
    table = table.astype(jnp.int32)
    dom_src = table[:, :leaves].reshape(box_dom, -1)
    dom_type = table[:, leaves : 2 * leaves].reshape(box_dom, -1)
    dom_csrc = table[:, 2 * leaves]
    dom_ctype = table[:, 2 * leaves + 1]

    domain_parents = jnp.einsum(
        "qce,cde->qd", domain.reshape(n_blk, leaves, coeffs), upward_translation_table, precision=top
    )
    parents = domain_parents
    carried = domain
    delivered = []
    mask = 1
    while mask < n_space:
        got = exchange(jnp.concatenate([carried, parents], axis=0), "space", mask)
        carried = got[:box_dom]
        delivered.append(carried)
        parents = jnp.concatenate([parents, got[box_dom:]], axis=0)
        mask *= 2
    all_parents = parents

    def neighbour(step):
        other = here + step
        pick = jnp.zeros_like(domain)
        for r, block in enumerate(delivered):
            pick = jnp.where((here ^ other) == 2 ** (r + 1) - 1, block, pick)
        inside = (other >= 0) & (other < n_space)
        return jnp.where(inside, pick, 0.0)

    window = jnp.concatenate([neighbour(-1), domain, neighbour(1)], axis=0)
    dom_csrc = (dom_csrc // n_blk ^ here) * n_blk + dom_csrc % n_blk

    src_hot = (dom_src[..., None] == jnp.arange(3 * box_dom, dtype=jnp.int32)).astype(jnp.bfloat16)
    type_hot = (dom_type[..., None] == jnp.arange(n_types, dtype=jnp.int32)).astype(jnp.bfloat16)
    counts = jnp.einsum("blt,blj->btj", type_hot, src_hot, preferred_element_type=jnp.float32)
    gathered = jnp.einsum("btj,jk->btk", counts, window, precision=top)
    n_parents = all_parents.shape[0]
    csrc_hot = (dom_csrc[..., None] == jnp.arange(n_parents, dtype=jnp.int32)).astype(jnp.bfloat16)
    ctype_hot = (dom_ctype[..., None] == jnp.arange(n_types, dtype=jnp.int32)).astype(jnp.bfloat16)
    ccounts = jnp.einsum("pet,peq->ptq", ctype_hot, csrc_hot, preferred_element_type=jnp.float32)
    cgathered = jnp.einsum("ptq,qk->ptk", ccounts, all_parents, precision=top)
    rows = jnp.concatenate([gathered, cgathered], axis=0)
    far = jnp.einsum("btk,tlk->bl", rows, translation, precision=top)
    leaf_far = far[:box_dom]
    parent_locals = far[box_dom:]
    downward = jnp.einsum(
        "qd,cds->qcs", parent_locals, upward_translation_table, precision=top
    ).reshape(box_dom, coeffs)
    domain_local = leaf_far + downward
    box_locals = lax.dynamic_slice_in_dim(domain_local, me * leaves, leaves, axis=0)
    block_locals = jnp.dot(box_hot, domain_local, precision=top)
    scaled = (bra_table.astype(jnp.float32) * block_locals[:, None, :]).astype(jnp.bfloat16)
    coulomb = jnp.einsum(
        "bmk,bnk->bmn", scaled, ket_table, preferred_element_type=jnp.float32
    ).astype(jnp.bfloat16)
    return (coulomb, box_locals)


def solution(mesh):
    placed = (
        P(("space", "blk"), None, None),
        P(("space", "blk"), None, None),
        P(("space", "blk"), None, None),
        P(("space", "blk")),
        P(("space", "blk"), None),
        P(("space", "blk"), None),
        P(("space", "blk"), None),
        P(("space", "blk"), None),
        P(),
        P(),
    )
    return jax.shard_map(
        shards,
        mesh=mesh,
        in_specs=placed,
        out_specs=(P(("space", "blk"), None, None), P(("space", "blk"), None)),
        check_vma=False,
    )
```

```python
import jax
import jax.numpy as jnp
from jax import lax
from jax.experimental import pallas as pl
from jax.experimental.pallas import tpu as pltpu
from jax.sharding import PartitionSpec as P

TILE = 8


def moments_kernel(dens_ref, bra_ref, ket_ref, out_ref):
    mixed = jnp.einsum(
        "bmn,bnk->bmk", dens_ref[...], ket_ref[...], preferred_element_type=jnp.float32
    )
    out_ref[...] = jnp.sum(bra_ref[...].astype(jnp.float32) * mixed, axis=1)


def block_moments(density, bra_table, ket_table):
    blocks, rows, cols = density.shape
    coeffs = bra_table.shape[2]
    return pl.pallas_call(
        moments_kernel,
        out_shape=jax.ShapeDtypeStruct((blocks, coeffs), jnp.float32),
        grid=(blocks // TILE,),
        in_specs=[
            pl.BlockSpec((TILE, rows, cols), lambda i: (i, 0, 0)),
            pl.BlockSpec((TILE, rows, coeffs), lambda i: (i, 0, 0)),
            pl.BlockSpec((TILE, cols, coeffs), lambda i: (i, 0, 0)),
        ],
        out_specs=pl.BlockSpec((TILE, coeffs), lambda i: (i, 0)),
        cost_estimate=pl.CostEstimate(
            flops=2 * blocks * rows * cols * coeffs,
            transcendentals=0,
            bytes_accessed=2 * blocks * (rows * cols + 2 * rows * coeffs) + 4 * blocks * coeffs,
        ),
    )(density, bra_table, ket_table)


def coulomb_kernel(bra_ref, ket_ref, local_ref, out_ref):
    scaled = (bra_ref[...].astype(jnp.float32) * local_ref[...][:, None, :]).astype(jnp.bfloat16)
    out_ref[...] = jnp.einsum(
        "bmk,bnk->bmn", scaled, ket_ref[...], preferred_element_type=jnp.float32
    ).astype(jnp.bfloat16)


def block_coulomb(bra_table, ket_table, block_locals):
    blocks, rows, coeffs = bra_table.shape
    cols = ket_table.shape[1]
    return pl.pallas_call(
        coulomb_kernel,
        out_shape=jax.ShapeDtypeStruct((blocks, rows, cols), jnp.bfloat16),
        grid=(blocks // TILE,),
        in_specs=[
            pl.BlockSpec((TILE, rows, coeffs), lambda i: (i, 0, 0)),
            pl.BlockSpec((TILE, cols, coeffs), lambda i: (i, 0, 0)),
            pl.BlockSpec((TILE, coeffs), lambda i: (i, 0)),
        ],
        out_specs=pl.BlockSpec((TILE, rows, cols), lambda i: (i, 0, 0)),
        cost_estimate=pl.CostEstimate(
            flops=2 * blocks * rows * cols * coeffs,
            transcendentals=0,
            bytes_accessed=2 * blocks * (rows * cols + 2 * rows * coeffs) + 4 * blocks * coeffs,
        ),
    )(bra_table, ket_table, block_locals)


def exchange(x, axis, mask):
    count = lax.axis_size(axis)
    return lax.ppermute(x, axis, [(i, i ^ mask) for i in range(count)])


def butterfly_sum(x, axis):
    count = lax.axis_size(axis)
    mask = 1
    while mask < count:
        x = x + exchange(x, axis, mask)
        mask *= 2
    return x


def butterfly_gather(x, axis):
    count = lax.axis_size(axis)
    me = lax.axis_index(axis)
    mask = 1
    while mask < count:
        other = exchange(x, axis, mask)
        low = (me // mask) % 2 == 0
        x = jnp.where(low, jnp.concatenate([x, other], 0), jnp.concatenate([other, x], 0))
        mask *= 2
    return x


def shards(
    density,
    bra_table,
    ket_table,
    box_of_block,
    leaf_src,
    leaf_type,
    coarse_src,
    coarse_type,
    translation,
    upward_translation_table,
):
    top = lax.Precision.HIGH
    n_blk = lax.axis_size("blk")
    n_space = lax.axis_size("space")
    me = lax.axis_index("blk")
    here = lax.axis_index("space")
    leaves = leaf_src.shape[0]
    box_dom = leaves * n_blk
    n_types = translation.shape[0]
    coeffs = translation.shape[1]

    lists = jnp.concatenate([leaf_src, leaf_type, coarse_src, coarse_type], axis=0)
    flat = lists.size
    table = jnp.zeros((n_blk, flat), jnp.float32)
    table = lax.dynamic_update_index_in_dim(table, lists.reshape(flat).astype(jnp.float32), me, 0)
    table_rows = -(-n_blk * flat // coeffs)
    table = jnp.pad(table.reshape(-1), (0, table_rows * coeffs - n_blk * flat))
    table = table.reshape(table_rows, coeffs)

    moments = block_moments(density, bra_table, ket_table)
    box_hot = (box_of_block[:, None] == jnp.arange(box_dom, dtype=jnp.int32)[None, :]).astype(
        jnp.float32
    )
    partial_moments = lax.dot_general(
        box_hot, moments, (((0,), (0,)), ((), ())), precision=top
    )
    summed = butterfly_sum(jnp.concatenate([partial_moments, table], axis=0), "blk")
    domain = summed[:box_dom]
    table = summed[box_dom:].reshape(-1)[: n_blk * flat].reshape((n_blk,) + lists.shape)
    table = table.astype(jnp.int32)
    dom_src = table[:, :leaves].reshape(box_dom, -1)
    dom_type = table[:, leaves : 2 * leaves].reshape(box_dom, -1)
    dom_csrc = table[:, 2 * leaves]
    dom_ctype = table[:, 2 * leaves + 1]

    domain_parents = jnp.einsum(
        "qce,cde->qd", domain.reshape(n_blk, leaves, coeffs), upward_translation_table, precision=top
    )
    parents = domain_parents
    carried = domain
    delivered = []
    mask = 1
    while mask < n_space:
        got = exchange(jnp.concatenate([carried, parents], axis=0), "space", mask)
        carried = got[:box_dom]
        delivered.append(carried)
        parents = jnp.concatenate([parents, got[box_dom:]], axis=0)
        mask *= 2
    all_parents = parents

    def neighbour(step):
        other = here + step
        pick = jnp.zeros_like(domain)
        for r, block in enumerate(delivered):
            pick = jnp.where((here ^ other) == 2 ** (r + 1) - 1, block, pick)
        inside = (other >= 0) & (other < n_space)
        return jnp.where(inside, pick, 0.0)

    window = jnp.concatenate([neighbour(-1), domain, neighbour(1)], axis=0)
    dom_csrc = (dom_csrc // n_blk ^ here) * n_blk + dom_csrc % n_blk

    src_hot = (dom_src[..., None] == jnp.arange(3 * box_dom, dtype=jnp.int32)).astype(jnp.bfloat16)
    type_hot = (dom_type[..., None] == jnp.arange(n_types, dtype=jnp.int32)).astype(jnp.bfloat16)
    counts = jnp.einsum("blt,blj->btj", type_hot, src_hot, preferred_element_type=jnp.float32)
    gathered = jnp.einsum("btj,jk->btk", counts, window, precision=top)
    n_parents = all_parents.shape[0]
    csrc_hot = (dom_csrc[..., None] == jnp.arange(n_parents, dtype=jnp.int32)).astype(jnp.bfloat16)
    ctype_hot = (dom_ctype[..., None] == jnp.arange(n_types, dtype=jnp.int32)).astype(jnp.bfloat16)
    ccounts = jnp.einsum("pet,peq->ptq", ctype_hot, csrc_hot, preferred_element_type=jnp.float32)
    cgathered = jnp.einsum("ptq,qk->ptk", ccounts, all_parents, precision=top)
    rows = jnp.concatenate([gathered, cgathered], axis=0)
    far = jnp.einsum("btk,tlk->bl", rows, translation, precision=top)
    leaf_far = far[:box_dom]
    parent_locals = far[box_dom:]
    downward = jnp.einsum(
        "qd,cds->qcs", parent_locals, upward_translation_table, precision=top
    ).reshape(box_dom, coeffs)
    domain_local = leaf_far + downward
    box_locals = lax.dynamic_slice_in_dim(domain_local, me * leaves, leaves, axis=0)
    block_locals = jnp.dot(box_hot, domain_local, precision=top)
    coulomb = block_coulomb(bra_table, ket_table, block_locals)
    return (coulomb, box_locals)


def solution(mesh):
    placed = (
        P(("space", "blk"), None, None),
        P(("space", "blk"), None, None),
        P(("space", "blk"), None, None),
        P(("space", "blk")),
        P(("space", "blk"), None),
        P(("space", "blk"), None),
        P(("space", "blk"), None),
        P(("space", "blk"), None),
        P(),
        P(),
    )
    return jax.shard_map(
        shards,
        mesh=mesh,
        in_specs=placed,
        out_specs=(P(("space", "blk"), None, None), P(("space", "blk"), None)),
        check_vma=False,
    )
```

```python
import jax
import jax.numpy as jnp
from jax import lax
from jax.experimental import pallas as pl
from jax.experimental.pallas import tpu as pltpu
from jax.sharding import PartitionSpec as P

def tile_of(blocks, most=48):
    for tile in range(most, 7, -8):
        if blocks % tile == 0:
            return tile
    return blocks


def moments_kernel(dens_ref, bra_ref, ket_ref, out_ref):
    for j in range(out_ref.shape[0]):
        mixed = jnp.dot(dens_ref[j], ket_ref[j], preferred_element_type=jnp.float32)
        out_ref[pl.ds(j, 1), :] = jnp.sum(
            bra_ref[j].astype(jnp.float32) * mixed, axis=0, keepdims=True
        )


def block_moments(density, bra_table, ket_table):
    blocks, rows, cols = density.shape
    coeffs = bra_table.shape[2]
    tile = tile_of(blocks)
    return pl.pallas_call(
        moments_kernel,
        out_shape=jax.ShapeDtypeStruct((blocks, coeffs), jnp.float32),
        grid=(blocks // tile,),
        in_specs=[
            pl.BlockSpec((tile, rows, cols), lambda i: (i, 0, 0)),
            pl.BlockSpec((tile, rows, coeffs), lambda i: (i, 0, 0)),
            pl.BlockSpec((tile, cols, coeffs), lambda i: (i, 0, 0)),
        ],
        out_specs=pl.BlockSpec((tile, coeffs), lambda i: (i, 0)),
        cost_estimate=pl.CostEstimate(
            flops=2 * blocks * rows * cols * coeffs,
            transcendentals=0,
            bytes_accessed=2 * blocks * (rows * cols + 2 * rows * coeffs) + 4 * blocks * coeffs,
        ),
    )(density, bra_table, ket_table)


def coulomb_kernel(bra_ref, ket_ref, local_ref, out_ref):
    for j in range(out_ref.shape[0]):
        scaled = (bra_ref[j].astype(jnp.float32) * local_ref[pl.ds(j, 1), :]).astype(jnp.bfloat16)
        out_ref[j] = lax.dot_general(
            scaled, ket_ref[j], (((1,), (1,)), ((), ())), preferred_element_type=jnp.float32
        ).astype(jnp.bfloat16)


def block_coulomb(bra_table, ket_table, block_locals):
    blocks, rows, coeffs = bra_table.shape
    cols = ket_table.shape[1]
    tile = tile_of(blocks)
    return pl.pallas_call(
        coulomb_kernel,
        out_shape=jax.ShapeDtypeStruct((blocks, rows, cols), jnp.bfloat16),
        grid=(blocks // tile,),
        in_specs=[
            pl.BlockSpec((tile, rows, coeffs), lambda i: (i, 0, 0)),
            pl.BlockSpec((tile, cols, coeffs), lambda i: (i, 0, 0)),
            pl.BlockSpec((tile, coeffs), lambda i: (i, 0)),
        ],
        out_specs=pl.BlockSpec((tile, rows, cols), lambda i: (i, 0, 0)),
        cost_estimate=pl.CostEstimate(
            flops=2 * blocks * rows * cols * coeffs,
            transcendentals=0,
            bytes_accessed=2 * blocks * (rows * cols + 2 * rows * coeffs) + 4 * blocks * coeffs,
        ),
    )(bra_table, ket_table, block_locals)


def exchange(x, axis, mask):
    count = lax.axis_size(axis)
    return lax.ppermute(x, axis, [(i, i ^ mask) for i in range(count)])


def butterfly_sum(x, axis):
    count = lax.axis_size(axis)
    mask = 1
    while mask < count:
        x = x + exchange(x, axis, mask)
        mask *= 2
    return x


def butterfly_gather(x, axis):
    count = lax.axis_size(axis)
    me = lax.axis_index(axis)
    mask = 1
    while mask < count:
        other = exchange(x, axis, mask)
        low = (me // mask) % 2 == 0
        x = jnp.where(low, jnp.concatenate([x, other], 0), jnp.concatenate([other, x], 0))
        mask *= 2
    return x


def shards(
    density,
    bra_table,
    ket_table,
    box_of_block,
    leaf_src,
    leaf_type,
    coarse_src,
    coarse_type,
    translation,
    upward_translation_table,
):
    top = lax.Precision.HIGH
    n_blk = lax.axis_size("blk")
    n_space = lax.axis_size("space")
    me = lax.axis_index("blk")
    here = lax.axis_index("space")
    leaves = leaf_src.shape[0]
    box_dom = leaves * n_blk
    n_types = translation.shape[0]
    coeffs = translation.shape[1]

    lists = jnp.concatenate([leaf_src, leaf_type, coarse_src, coarse_type], axis=0)
    flat = lists.size
    table = jnp.zeros((n_blk, flat), jnp.float32)
    table = lax.dynamic_update_index_in_dim(table, lists.reshape(flat).astype(jnp.float32), me, 0)
    table_rows = -(-n_blk * flat // coeffs)
    table = jnp.pad(table.reshape(-1), (0, table_rows * coeffs - n_blk * flat))
    table = table.reshape(table_rows, coeffs)

    moments = block_moments(density, bra_table, ket_table)
    box_hot = (box_of_block[:, None] == jnp.arange(box_dom, dtype=jnp.int32)[None, :]).astype(
        jnp.float32
    )
    partial_moments = lax.dot_general(
        box_hot, moments, (((0,), (0,)), ((), ())), precision=top
    )
    summed = butterfly_sum(jnp.concatenate([partial_moments, table], axis=0), "blk")
    domain = summed[:box_dom]
    table = summed[box_dom:].reshape(-1)[: n_blk * flat].reshape((n_blk,) + lists.shape)
    table = table.astype(jnp.int32)
    dom_src = table[:, :leaves].reshape(box_dom, -1)
    dom_type = table[:, leaves : 2 * leaves].reshape(box_dom, -1)
    dom_csrc = table[:, 2 * leaves]
    dom_ctype = table[:, 2 * leaves + 1]

    domain_parents = jnp.einsum(
        "qce,cde->qd", domain.reshape(n_blk, leaves, coeffs), upward_translation_table, precision=top
    )
    parents = domain_parents
    carried = domain
    delivered = []
    mask = 1
    while mask < n_space:
        got = exchange(jnp.concatenate([carried, parents], axis=0), "space", mask)
        carried = got[:box_dom]
        delivered.append(carried)
        parents = jnp.concatenate([parents, got[box_dom:]], axis=0)
        mask *= 2
    all_parents = parents

    def neighbour(step):
        other = here + step
        pick = jnp.zeros_like(domain)
        for r, block in enumerate(delivered):
            pick = jnp.where((here ^ other) == 2 ** (r + 1) - 1, block, pick)
        inside = (other >= 0) & (other < n_space)
        return jnp.where(inside, pick, 0.0)

    window = jnp.concatenate([neighbour(-1), domain, neighbour(1)], axis=0)
    dom_csrc = (dom_csrc // n_blk ^ here) * n_blk + dom_csrc % n_blk

    src_hot = (dom_src[..., None] == jnp.arange(3 * box_dom, dtype=jnp.int32)).astype(jnp.bfloat16)
    type_hot = (dom_type[..., None] == jnp.arange(n_types, dtype=jnp.int32)).astype(jnp.bfloat16)
    counts = jnp.einsum("blt,blj->btj", type_hot, src_hot, preferred_element_type=jnp.float32)
    gathered = jnp.einsum("btj,jk->btk", counts, window, precision=top)
    n_parents = all_parents.shape[0]
    csrc_hot = (dom_csrc[..., None] == jnp.arange(n_parents, dtype=jnp.int32)).astype(jnp.bfloat16)
    ctype_hot = (dom_ctype[..., None] == jnp.arange(n_types, dtype=jnp.int32)).astype(jnp.bfloat16)
    ccounts = jnp.einsum("pet,peq->ptq", ctype_hot, csrc_hot, preferred_element_type=jnp.float32)
    cgathered = jnp.einsum("ptq,qk->ptk", ccounts, all_parents, precision=top)
    rows = jnp.concatenate([gathered, cgathered], axis=0)
    far = jnp.einsum("btk,tlk->bl", rows, translation, precision=top)
    leaf_far = far[:box_dom]
    parent_locals = far[box_dom:]
    downward = jnp.einsum(
        "qd,cds->qcs", parent_locals, upward_translation_table, precision=top
    ).reshape(box_dom, coeffs)
    domain_local = leaf_far + downward
    box_locals = lax.dynamic_slice_in_dim(domain_local, me * leaves, leaves, axis=0)
    block_locals = jnp.dot(box_hot, domain_local, precision=top)
    coulomb = block_coulomb(bra_table, ket_table, block_locals)
    return (coulomb, box_locals)


def solution(mesh):
    placed = (
        P(("space", "blk"), None, None),
        P(("space", "blk"), None, None),
        P(("space", "blk"), None, None),
        P(("space", "blk")),
        P(("space", "blk"), None),
        P(("space", "blk"), None),
        P(("space", "blk"), None),
        P(("space", "blk"), None),
        P(),
        P(),
    )
    return jax.shard_map(
        shards,
        mesh=mesh,
        in_specs=placed,
        out_specs=(P(("space", "blk"), None, None), P(("space", "blk"), None)),
        check_vma=False,
    )
```

```python
import jax
import jax.numpy as jnp
from jax import lax
from jax.experimental import pallas as pl
from jax.experimental.pallas import tpu as pltpu
from jax.sharding import PartitionSpec as P

def tile_of(blocks, most=48):
    for tile in range(most, 7, -8):
        if blocks % tile == 0:
            return tile
    return blocks


def moments_kernel(dens_ref, bra_ref, ket_ref, out_ref):
    for j in range(out_ref.shape[0]):
        mixed = jnp.dot(dens_ref[j], ket_ref[j], preferred_element_type=jnp.float32)
        out_ref[pl.ds(j, 1), :] = jnp.sum(
            bra_ref[j].astype(jnp.float32) * mixed, axis=0, keepdims=True
        )


def block_moments(density, bra_table, ket_table):
    blocks, rows, cols = density.shape
    coeffs = bra_table.shape[2]
    tile = tile_of(blocks)
    return pl.pallas_call(
        moments_kernel,
        out_shape=jax.ShapeDtypeStruct((blocks, coeffs), jnp.float32),
        grid=(blocks // tile,),
        in_specs=[
            pl.BlockSpec((tile, rows, cols), lambda i: (i, 0, 0)),
            pl.BlockSpec((tile, rows, coeffs), lambda i: (i, 0, 0)),
            pl.BlockSpec((tile, cols, coeffs), lambda i: (i, 0, 0)),
        ],
        out_specs=pl.BlockSpec((tile, coeffs), lambda i: (i, 0)),
        cost_estimate=pl.CostEstimate(
            flops=2 * blocks * rows * cols * coeffs,
            transcendentals=0,
            bytes_accessed=2 * blocks * (rows * cols + 2 * rows * coeffs) + 4 * blocks * coeffs,
        ),
    )(density, bra_table, ket_table)


def coulomb_kernel(bra_ref, ket_ref, local_ref, out_ref):
    for j in range(out_ref.shape[0]):
        scaled = (bra_ref[j].astype(jnp.float32) * local_ref[pl.ds(j, 1), :]).astype(jnp.bfloat16)
        out_ref[j] = lax.dot_general(
            scaled, ket_ref[j], (((1,), (1,)), ((), ())), preferred_element_type=jnp.float32
        ).astype(jnp.bfloat16)


def block_coulomb(bra_table, ket_table, block_locals):
    blocks, rows, coeffs = bra_table.shape
    cols = ket_table.shape[1]
    tile = tile_of(blocks)
    return pl.pallas_call(
        coulomb_kernel,
        out_shape=jax.ShapeDtypeStruct((blocks, rows, cols), jnp.bfloat16),
        grid=(blocks // tile,),
        in_specs=[
            pl.BlockSpec((tile, rows, coeffs), lambda i: (i, 0, 0)),
            pl.BlockSpec((tile, cols, coeffs), lambda i: (i, 0, 0)),
            pl.BlockSpec((tile, coeffs), lambda i: (i, 0)),
        ],
        out_specs=pl.BlockSpec((tile, rows, cols), lambda i: (i, 0, 0)),
        cost_estimate=pl.CostEstimate(
            flops=2 * blocks * rows * cols * coeffs,
            transcendentals=0,
            bytes_accessed=2 * blocks * (rows * cols + 2 * rows * coeffs) + 4 * blocks * coeffs,
        ),
    )(bra_table, ket_table, block_locals)


def exchange(x, axis, mask):
    count = lax.axis_size(axis)
    return lax.ppermute(x, axis, [(i, i ^ mask) for i in range(count)])


def joint(x, target_of):
    n_space = lax.axis_size("space")
    n_blk = lax.axis_size("blk")
    pairs = []
    for a in range(n_space):
        for b in range(n_blk):
            ta, tb = target_of(a, b)
            pairs.append((a * n_blk + b, ta * n_blk + tb))
    return lax.ppermute(x, ("space", "blk"), pairs)


def two_port(x, first, second, axis):
    n_blk = lax.axis_size("blk")
    chips = n_blk // 2 if axis == "blk" else lax.axis_size("space")

    def target_of(a, b):
        step = first if b % 2 == 0 else second
        if axis == "blk":
            return a, 2 * ((b // 2 + step) % chips) + b % 2
        return (a + step) % chips, b

    got = joint(x, target_of)
    other = exchange(got, "blk", 1)
    core0 = lax.axis_index("blk") % 2 == 0
    return jnp.where(core0, got, other), jnp.where(core0, other, got)


def chip_sum(x):
    chip = x + exchange(x, "blk", 1)
    behind1, behind2 = two_port(chip, 1, 2, "blk")
    pair = chip + behind1
    three = pair + behind2
    core0 = lax.axis_index("blk") % 2 == 0
    behind3, behind6 = two_port(jnp.where(core0, three, pair), 3, 6, "blk")
    return (three + behind3) + behind6


def butterfly_sum(x, axis):
    count = lax.axis_size(axis)
    mask = 1
    while mask < count:
        x = x + exchange(x, axis, mask)
        mask *= 2
    return x


def butterfly_gather(x, axis):
    count = lax.axis_size(axis)
    me = lax.axis_index(axis)
    mask = 1
    while mask < count:
        other = exchange(x, axis, mask)
        low = (me // mask) % 2 == 0
        x = jnp.where(low, jnp.concatenate([x, other], 0), jnp.concatenate([other, x], 0))
        mask *= 2
    return x


def shards(
    density,
    bra_table,
    ket_table,
    box_of_block,
    leaf_src,
    leaf_type,
    coarse_src,
    coarse_type,
    translation,
    upward_translation_table,
):
    top = lax.Precision.HIGH
    n_blk = lax.axis_size("blk")
    n_space = lax.axis_size("space")
    me = lax.axis_index("blk")
    here = lax.axis_index("space")
    leaves = leaf_src.shape[0]
    box_dom = leaves * n_blk
    n_types = translation.shape[0]
    coeffs = translation.shape[1]

    lists = jnp.concatenate([leaf_src, leaf_type, coarse_src, coarse_type], axis=0)
    flat = lists.size
    table = jnp.zeros((n_blk, flat), jnp.float32)
    table = lax.dynamic_update_index_in_dim(table, lists.reshape(flat).astype(jnp.float32), me, 0)
    table_rows = -(-n_blk * flat // coeffs)
    table = jnp.pad(table.reshape(-1), (0, table_rows * coeffs - n_blk * flat))
    table = table.reshape(table_rows, coeffs)

    moments = block_moments(density, bra_table, ket_table)
    box_hot = (box_of_block[:, None] == jnp.arange(box_dom, dtype=jnp.int32)[None, :]).astype(
        jnp.float32
    )
    partial_moments = lax.dot_general(
        box_hot, moments, (((0,), (0,)), ((), ())), precision=top
    )
    stacked = jnp.concatenate([partial_moments, table], axis=0)
    if n_blk == 16:
        summed = chip_sum(stacked)
    else:
        summed = butterfly_sum(stacked, "blk")
    domain = summed[:box_dom]
    table = summed[box_dom:].reshape(-1)[: n_blk * flat].reshape((n_blk,) + lists.shape)
    table = table.astype(jnp.int32)
    dom_src = table[:, :leaves].reshape(box_dom, -1)
    dom_type = table[:, leaves : 2 * leaves].reshape(box_dom, -1)
    dom_csrc = table[:, 2 * leaves]
    dom_ctype = table[:, 2 * leaves + 1]

    domain_parents = jnp.einsum(
        "qce,cde->qd", domain.reshape(n_blk, leaves, coeffs), upward_translation_table, precision=top
    )
    if n_space == 8 and n_blk % 2 == 0:
        first = jnp.concatenate([domain, domain_parents], axis=0)
        behind1, behind2 = two_port(first, 1, 2, "space")
        low_block = behind1[:box_dom]
        parents = jnp.concatenate([domain_parents, behind1[box_dom:], behind2[box_dom:]], axis=0)
        second = jnp.concatenate([low_block, parents], axis=0)
        behind3, behind6 = two_port(second, 3, 6, "space")
        high_block = behind6[:box_dom]
        all_parents = jnp.concatenate(
            [parents, behind3[box_dom:], behind6[box_dom : box_dom + 2 * n_blk]], axis=0
        )
        low = jnp.where(here > 0, low_block, 0.0)
        high = jnp.where(here < n_space - 1, high_block, 0.0)
        window = jnp.concatenate([low, domain, high], axis=0)
        dom_csrc = ((here - dom_csrc // n_blk) % n_space) * n_blk + dom_csrc % n_blk
    else:
        parents = domain_parents
        carried = domain
        delivered = []
        mask = 1
        while mask < n_space:
            got = exchange(jnp.concatenate([carried, parents], axis=0), "space", mask)
            carried = got[:box_dom]
            delivered.append(carried)
            parents = jnp.concatenate([parents, got[box_dom:]], axis=0)
            mask *= 2
        all_parents = parents

        def neighbour(step):
            other = here + step
            pick = jnp.zeros_like(domain)
            for r, block in enumerate(delivered):
                pick = jnp.where((here ^ other) == 2 ** (r + 1) - 1, block, pick)
            inside = (other >= 0) & (other < n_space)
            return jnp.where(inside, pick, 0.0)

        window = jnp.concatenate([neighbour(-1), domain, neighbour(1)], axis=0)
        dom_csrc = (dom_csrc // n_blk ^ here) * n_blk + dom_csrc % n_blk

    src_hot = (dom_src[..., None] == jnp.arange(3 * box_dom, dtype=jnp.int32)).astype(jnp.bfloat16)
    type_hot = (dom_type[..., None] == jnp.arange(n_types, dtype=jnp.int32)).astype(jnp.bfloat16)
    counts = jnp.einsum("blt,blj->btj", type_hot, src_hot, preferred_element_type=jnp.float32)
    gathered = jnp.einsum("btj,jk->btk", counts, window, precision=top)
    n_parents = all_parents.shape[0]
    csrc_hot = (dom_csrc[..., None] == jnp.arange(n_parents, dtype=jnp.int32)).astype(jnp.bfloat16)
    ctype_hot = (dom_ctype[..., None] == jnp.arange(n_types, dtype=jnp.int32)).astype(jnp.bfloat16)
    ccounts = jnp.einsum("pet,peq->ptq", ctype_hot, csrc_hot, preferred_element_type=jnp.float32)
    cgathered = jnp.einsum("ptq,qk->ptk", ccounts, all_parents, precision=top)
    rows = jnp.concatenate([gathered, cgathered], axis=0)
    far = jnp.einsum("btk,tlk->bl", rows, translation, precision=top)
    leaf_far = far[:box_dom]
    parent_locals = far[box_dom:]
    downward = jnp.einsum(
        "qd,cds->qcs", parent_locals, upward_translation_table, precision=top
    ).reshape(box_dom, coeffs)
    domain_local = leaf_far + downward
    box_locals = lax.dynamic_slice_in_dim(domain_local, me * leaves, leaves, axis=0)
    block_locals = jnp.dot(box_hot, domain_local, precision=top)
    coulomb = block_coulomb(bra_table, ket_table, block_locals)
    return (coulomb, box_locals)


def solution(mesh):
    placed = (
        P(("space", "blk"), None, None),
        P(("space", "blk"), None, None),
        P(("space", "blk"), None, None),
        P(("space", "blk")),
        P(("space", "blk"), None),
        P(("space", "blk"), None),
        P(("space", "blk"), None),
        P(("space", "blk"), None),
        P(),
        P(),
    )
    return jax.shard_map(
        shards,
        mesh=mesh,
        in_specs=placed,
        out_specs=(P(("space", "blk"), None, None), P(("space", "blk"), None)),
        check_vma=False,
    )
```

```python
import jax
import jax.numpy as jnp
from jax import lax
from jax.experimental import pallas as pl
from jax.experimental.pallas import tpu as pltpu
from jax.sharding import PartitionSpec as P

def tile_of(blocks, most=48):
    for tile in range(most, 7, -8):
        if blocks % tile == 0:
            return tile
    return blocks


def moments_kernel(dens_ref, bra_ref, ket_ref, out_ref):
    for j in range(out_ref.shape[0]):
        mixed = jnp.dot(dens_ref[j], ket_ref[j], preferred_element_type=jnp.float32)
        out_ref[pl.ds(j, 1), :] = jnp.sum(
            bra_ref[j].astype(jnp.float32) * mixed, axis=0, keepdims=True
        )


def block_moments(density, bra_table, ket_table):
    blocks, rows, cols = density.shape
    coeffs = bra_table.shape[2]
    tile = tile_of(blocks)
    return pl.pallas_call(
        moments_kernel,
        out_shape=jax.ShapeDtypeStruct((blocks, coeffs), jnp.float32),
        grid=(blocks // tile,),
        in_specs=[
            pl.BlockSpec((tile, rows, cols), lambda i: (i, 0, 0)),
            pl.BlockSpec((tile, rows, coeffs), lambda i: (i, 0, 0)),
            pl.BlockSpec((tile, cols, coeffs), lambda i: (i, 0, 0)),
        ],
        out_specs=pl.BlockSpec((tile, coeffs), lambda i: (i, 0)),
        cost_estimate=pl.CostEstimate(
            flops=2 * blocks * rows * cols * coeffs,
            transcendentals=0,
            bytes_accessed=2 * blocks * (rows * cols + 2 * rows * coeffs) + 4 * blocks * coeffs,
        ),
    )(density, bra_table, ket_table)


def coulomb_kernel(bra_ref, ket_ref, local_ref, out_ref):
    for j in range(out_ref.shape[0]):
        scaled = (bra_ref[j].astype(jnp.float32) * local_ref[pl.ds(j, 1), :]).astype(jnp.bfloat16)
        out_ref[j] = lax.dot_general(
            scaled, ket_ref[j], (((1,), (1,)), ((), ())), preferred_element_type=jnp.float32
        ).astype(jnp.bfloat16)


def block_coulomb(bra_table, ket_table, block_locals):
    blocks, rows, coeffs = bra_table.shape
    cols = ket_table.shape[1]
    tile = tile_of(blocks)
    return pl.pallas_call(
        coulomb_kernel,
        out_shape=jax.ShapeDtypeStruct((blocks, rows, cols), jnp.bfloat16),
        grid=(blocks // tile,),
        in_specs=[
            pl.BlockSpec((tile, rows, coeffs), lambda i: (i, 0, 0)),
            pl.BlockSpec((tile, cols, coeffs), lambda i: (i, 0, 0)),
            pl.BlockSpec((tile, coeffs), lambda i: (i, 0)),
        ],
        out_specs=pl.BlockSpec((tile, rows, cols), lambda i: (i, 0, 0)),
        cost_estimate=pl.CostEstimate(
            flops=2 * blocks * rows * cols * coeffs,
            transcendentals=0,
            bytes_accessed=2 * blocks * (rows * cols + 2 * rows * coeffs) + 4 * blocks * coeffs,
        ),
    )(bra_table, ket_table, block_locals)


def exchange(x, axis, mask):
    count = lax.axis_size(axis)
    return lax.ppermute(x, axis, [(i, i ^ mask) for i in range(count)])


def butterfly_sum(x, axis):
    count = lax.axis_size(axis)
    mask = 1
    while mask < count:
        x = x + exchange(x, axis, mask)
        mask *= 2
    return x


def butterfly_gather(x, axis):
    count = lax.axis_size(axis)
    me = lax.axis_index(axis)
    mask = 1
    while mask < count:
        other = exchange(x, axis, mask)
        low = (me // mask) % 2 == 0
        x = jnp.where(low, jnp.concatenate([x, other], 0), jnp.concatenate([other, x], 0))
        mask *= 2
    return x


def shards(
    density,
    bra_table,
    ket_table,
    box_of_block,
    leaf_src,
    leaf_type,
    coarse_src,
    coarse_type,
    translation,
    upward_translation_table,
):
    top = lax.Precision.HIGH
    n_blk = lax.axis_size("blk")
    n_space = lax.axis_size("space")
    me = lax.axis_index("blk")
    here = lax.axis_index("space")
    leaves = leaf_src.shape[0]
    box_dom = leaves * n_blk
    n_types = translation.shape[0]
    coeffs = translation.shape[1]

    core = me % 2
    core0 = core == 0
    half = box_dom // 2

    lists = jnp.concatenate([leaf_src, leaf_type, coarse_src, coarse_type], axis=0)
    flat = lists.size
    table = jnp.zeros((n_blk, flat), jnp.float32)
    table = lax.dynamic_update_index_in_dim(table, lists.reshape(flat).astype(jnp.float32), me, 0)
    table_rows = 2 * -(-n_blk * flat // (2 * coeffs))
    table = jnp.pad(table.reshape(-1), (0, table_rows * coeffs - n_blk * flat))
    table = table.reshape(table_rows, coeffs)
    t_half = table_rows // 2

    moments = block_moments(density, bra_table, ket_table)
    box_hot = (box_of_block[:, None] == jnp.arange(box_dom, dtype=jnp.int32)[None, :]).astype(
        jnp.float32
    )
    partial_moments = lax.dot_general(
        box_hot, moments, (((0,), (0,)), ((), ())), precision=top
    )
    first = jnp.concatenate([partial_moments[:half], table[:t_half]], axis=0)
    second = jnp.concatenate([partial_moments[half:], table[t_half:]], axis=0)
    mine = jnp.where(core0, first, second)
    summed = mine + exchange(jnp.where(core0, second, first), "blk", 1)
    mask = 2
    while mask < n_blk:
        summed = summed + exchange(summed, "blk", mask)
        mask *= 2
    leaf_half = summed[:half]
    table_half = summed[half:]

    parent_half = jnp.einsum(
        "qce,cde->qd", leaf_half.reshape(-1, 8, coeffs), upward_translation_table, precision=top
    )
    p_half = parent_half.shape[0]
    parents = parent_half
    carried = leaf_half
    delivered = []
    mask = 1
    while mask < n_space:
        got = exchange(jnp.concatenate([carried, parents], axis=0), "space", mask)
        carried = got[:half]
        delivered.append(carried)
        parents = jnp.concatenate([parents, got[half:]], axis=0)
        mask *= 2

    def neighbour(step):
        other = here + step
        pick = jnp.zeros_like(leaf_half)
        for r, block in enumerate(delivered):
            pick = jnp.where((here ^ other) == 2 ** (r + 1) - 1, block, pick)
        inside = (other >= 0) & (other < n_space)
        return jnp.where(inside, pick, 0.0)

    own = jnp.concatenate([neighbour(-1), leaf_half, neighbour(1), parents, table_half], axis=0)
    theirs = exchange(own, "blk", 1)
    low_part = jnp.where(core0, own, theirs)
    high_part = jnp.where(core0, theirs, own)

    def joined(start, size):
        return jnp.concatenate(
            [low_part[start : start + size], high_part[start : start + size]], axis=0
        )

    window = jnp.concatenate([joined(0, half), joined(half, half), joined(2 * half, half)], axis=0)
    domain = joined(half, half)
    slots = parents.shape[0] // p_half
    all_parents = jnp.concatenate(
        [joined(3 * half + j * p_half, p_half) for j in range(slots)], axis=0
    )
    table = joined(3 * half + slots * p_half, t_half)
    table = table.reshape(-1)[: n_blk * flat].reshape((n_blk,) + lists.shape)
    table = table.astype(jnp.int32)
    dom_src = table[:, :leaves].reshape(box_dom, -1)
    dom_type = table[:, leaves : 2 * leaves].reshape(box_dom, -1)
    dom_csrc = table[:, 2 * leaves]
    dom_ctype = table[:, 2 * leaves + 1]
    dom_csrc = (dom_csrc // n_blk ^ here) * n_blk + dom_csrc % n_blk
    del domain

    src_hot = (dom_src[..., None] == jnp.arange(3 * box_dom, dtype=jnp.int32)).astype(jnp.bfloat16)
    type_hot = (dom_type[..., None] == jnp.arange(n_types, dtype=jnp.int32)).astype(jnp.bfloat16)
    counts = jnp.einsum("blt,blj->btj", type_hot, src_hot, preferred_element_type=jnp.float32)
    gathered = jnp.einsum("btj,jk->btk", counts, window, precision=top)
    n_parents = all_parents.shape[0]
    csrc_hot = (dom_csrc[..., None] == jnp.arange(n_parents, dtype=jnp.int32)).astype(jnp.bfloat16)
    ctype_hot = (dom_ctype[..., None] == jnp.arange(n_types, dtype=jnp.int32)).astype(jnp.bfloat16)
    ccounts = jnp.einsum("pet,peq->ptq", ctype_hot, csrc_hot, preferred_element_type=jnp.float32)
    cgathered = jnp.einsum("ptq,qk->ptk", ccounts, all_parents, precision=top)
    rows = jnp.concatenate([gathered, cgathered], axis=0)
    far = jnp.einsum("btk,tlk->bl", rows, translation, precision=top)
    leaf_far = far[:box_dom]
    parent_locals = far[box_dom:]
    downward = jnp.einsum(
        "qd,cds->qcs", parent_locals, upward_translation_table, precision=top
    ).reshape(box_dom, coeffs)
    domain_local = leaf_far + downward
    box_locals = lax.dynamic_slice_in_dim(domain_local, me * leaves, leaves, axis=0)
    block_locals = jnp.dot(box_hot, domain_local, precision=top)
    coulomb = block_coulomb(bra_table, ket_table, block_locals)
    return (coulomb, box_locals)


def solution(mesh):
    placed = (
        P(("space", "blk"), None, None),
        P(("space", "blk"), None, None),
        P(("space", "blk"), None, None),
        P(("space", "blk")),
        P(("space", "blk"), None),
        P(("space", "blk"), None),
        P(("space", "blk"), None),
        P(("space", "blk"), None),
        P(),
        P(),
    )
    return jax.shard_map(
        shards,
        mesh=mesh,
        in_specs=placed,
        out_specs=(P(("space", "blk"), None, None), P(("space", "blk"), None)),
        check_vma=False,
    )
```

```python
import jax
import jax.numpy as jnp
from jax import lax
from jax.experimental import pallas as pl
from jax.experimental.pallas import tpu as pltpu
from jax.sharding import PartitionSpec as P

def tile_of(blocks, most=48):
    for tile in range(most, 7, -8):
        if blocks % tile == 0:
            return tile
    return blocks


def moments_kernel(dens_ref, bra_ref, ket_ref, out_ref):
    for j in range(out_ref.shape[0]):
        mixed = jnp.dot(dens_ref[j], ket_ref[j], preferred_element_type=jnp.float32)
        out_ref[pl.ds(j, 1), :] = jnp.sum(
            bra_ref[j].astype(jnp.float32) * mixed, axis=0, keepdims=True
        )


def block_moments(density, bra_table, ket_table):
    blocks, rows, cols = density.shape
    coeffs = bra_table.shape[2]
    tile = tile_of(blocks)
    return pl.pallas_call(
        moments_kernel,
        out_shape=jax.ShapeDtypeStruct((blocks, coeffs), jnp.float32),
        grid=(blocks // tile,),
        in_specs=[
            pl.BlockSpec((tile, rows, cols), lambda i: (i, 0, 0)),
            pl.BlockSpec((tile, rows, coeffs), lambda i: (i, 0, 0)),
            pl.BlockSpec((tile, cols, coeffs), lambda i: (i, 0, 0)),
        ],
        out_specs=pl.BlockSpec((tile, coeffs), lambda i: (i, 0)),
        cost_estimate=pl.CostEstimate(
            flops=2 * blocks * rows * cols * coeffs,
            transcendentals=0,
            bytes_accessed=2 * blocks * (rows * cols + 2 * rows * coeffs) + 4 * blocks * coeffs,
        ),
    )(density, bra_table, ket_table)


def coulomb_kernel(bra_ref, ket_ref, local_ref, out_ref):
    for j in range(out_ref.shape[0]):
        scaled = (bra_ref[j].astype(jnp.float32) * local_ref[pl.ds(j, 1), :]).astype(jnp.bfloat16)
        out_ref[j] = lax.dot_general(
            scaled, ket_ref[j], (((1,), (1,)), ((), ())), preferred_element_type=jnp.float32
        ).astype(jnp.bfloat16)


def block_coulomb(bra_table, ket_table, block_locals):
    blocks, rows, coeffs = bra_table.shape
    cols = ket_table.shape[1]
    tile = tile_of(blocks)
    return pl.pallas_call(
        coulomb_kernel,
        out_shape=jax.ShapeDtypeStruct((blocks, rows, cols), jnp.bfloat16),
        grid=(blocks // tile,),
        in_specs=[
            pl.BlockSpec((tile, rows, coeffs), lambda i: (i, 0, 0)),
            pl.BlockSpec((tile, cols, coeffs), lambda i: (i, 0, 0)),
            pl.BlockSpec((tile, coeffs), lambda i: (i, 0)),
        ],
        out_specs=pl.BlockSpec((tile, rows, cols), lambda i: (i, 0, 0)),
        cost_estimate=pl.CostEstimate(
            flops=2 * blocks * rows * cols * coeffs,
            transcendentals=0,
            bytes_accessed=2 * blocks * (rows * cols + 2 * rows * coeffs) + 4 * blocks * coeffs,
        ),
    )(bra_table, ket_table, block_locals)


def exchange(x, axis, mask):
    count = lax.axis_size(axis)
    return lax.ppermute(x, axis, [(i, i ^ mask) for i in range(count)])


def butterfly_sum(x, axis):
    count = lax.axis_size(axis)
    mask = 1
    while mask < count:
        x = x + exchange(x, axis, mask)
        mask *= 2
    return x


def butterfly_gather(x, axis):
    count = lax.axis_size(axis)
    me = lax.axis_index(axis)
    mask = 1
    while mask < count:
        other = exchange(x, axis, mask)
        low = (me // mask) % 2 == 0
        x = jnp.where(low, jnp.concatenate([x, other], 0), jnp.concatenate([other, x], 0))
        mask *= 2
    return x


def shards(
    density,
    bra_table,
    ket_table,
    box_of_block,
    leaf_src,
    leaf_type,
    coarse_src,
    coarse_type,
    translation,
    upward_translation_table,
):
    top = lax.Precision.HIGH
    n_blk = lax.axis_size("blk")
    n_space = lax.axis_size("space")
    me = lax.axis_index("blk")
    here = lax.axis_index("space")
    leaves = leaf_src.shape[0]
    box_dom = leaves * n_blk
    n_types = translation.shape[0]
    coeffs = translation.shape[1]

    core = me % 2
    core0 = core == 0
    half = box_dom // 2

    lists = jnp.concatenate([leaf_src, leaf_type, coarse_src, coarse_type], axis=0)
    flat = lists.size
    table = jnp.zeros((n_blk, flat), jnp.float32)
    table = lax.dynamic_update_index_in_dim(table, lists.reshape(flat).astype(jnp.float32), me, 0)
    table_rows = 2 * -(-n_blk * flat // (2 * coeffs))
    table = jnp.pad(table.reshape(-1), (0, table_rows * coeffs - n_blk * flat))
    table = table.reshape(table_rows, coeffs)

    moments = block_moments(density, bra_table, ket_table)
    box_hot = (box_of_block[:, None] == jnp.arange(box_dom, dtype=jnp.int32)[None, :]).astype(
        jnp.float32
    )
    partial_moments = lax.dot_general(
        box_hot, moments, (((0,), (0,)), ((), ())), precision=top
    )
    first = jnp.concatenate([partial_moments[:half], table], axis=0)
    second = jnp.concatenate([partial_moments[half:], table], axis=0)
    mine = jnp.where(core0, first, second)
    summed = mine + exchange(jnp.where(core0, second, first), "blk", 1)
    mask = 2
    while mask < n_blk:
        summed = summed + exchange(summed, "blk", mask)
        mask *= 2
    leaf_half = summed[:half]
    table = summed[half:]

    parent_half = jnp.einsum(
        "qce,cde->qd", leaf_half.reshape(-1, 8, coeffs), upward_translation_table, precision=top
    )
    p_half = parent_half.shape[0]
    parents = parent_half
    carried = leaf_half
    delivered = []
    mask = 1
    while mask < n_space:
        got = exchange(jnp.concatenate([carried, parents], axis=0), "space", mask)
        carried = got[:half]
        delivered.append(carried)
        parents = jnp.concatenate([parents, got[half:]], axis=0)
        mask *= 2

    def neighbour(step):
        other = here + step
        pick = jnp.zeros_like(leaf_half)
        for r, block in enumerate(delivered):
            pick = jnp.where((here ^ other) == 2 ** (r + 1) - 1, block, pick)
        inside = (other >= 0) & (other < n_space)
        return jnp.where(inside, pick, 0.0)

    own = jnp.concatenate([neighbour(-1), leaf_half, neighbour(1), parents], axis=0)
    theirs = exchange(own, "blk", 1)
    low_part = jnp.where(core0, own, theirs)
    high_part = jnp.where(core0, theirs, own)

    def joined(start, size):
        return jnp.concatenate(
            [low_part[start : start + size], high_part[start : start + size]], axis=0
        )

    window = jnp.concatenate([joined(0, half), joined(half, half), joined(2 * half, half)], axis=0)
    domain = joined(half, half)
    slots = parents.shape[0] // p_half
    all_parents = jnp.concatenate(
        [joined(3 * half + j * p_half, p_half) for j in range(slots)], axis=0
    )
    table = table.reshape(-1)[: n_blk * flat].reshape((n_blk,) + lists.shape)
    table = table.astype(jnp.int32)
    dom_src = table[:, :leaves].reshape(box_dom, -1)
    dom_type = table[:, leaves : 2 * leaves].reshape(box_dom, -1)
    dom_csrc = table[:, 2 * leaves]
    dom_ctype = table[:, 2 * leaves + 1]
    dom_csrc = (dom_csrc // n_blk ^ here) * n_blk + dom_csrc % n_blk
    del domain

    src_hot = (dom_src[..., None] == jnp.arange(3 * box_dom, dtype=jnp.int32)).astype(jnp.bfloat16)
    type_hot = (dom_type[..., None] == jnp.arange(n_types, dtype=jnp.int32)).astype(jnp.bfloat16)
    counts = jnp.einsum("blt,blj->btj", type_hot, src_hot, preferred_element_type=jnp.float32)
    gathered = jnp.einsum("btj,jk->btk", counts, window, precision=top)
    n_parents = all_parents.shape[0]
    csrc_hot = (dom_csrc[..., None] == jnp.arange(n_parents, dtype=jnp.int32)).astype(jnp.bfloat16)
    ctype_hot = (dom_ctype[..., None] == jnp.arange(n_types, dtype=jnp.int32)).astype(jnp.bfloat16)
    ccounts = jnp.einsum("pet,peq->ptq", ctype_hot, csrc_hot, preferred_element_type=jnp.float32)
    cgathered = jnp.einsum("ptq,qk->ptk", ccounts, all_parents, precision=top)
    rows = jnp.concatenate([gathered, cgathered], axis=0)
    far = jnp.einsum("btk,tlk->bl", rows, translation, precision=top)
    leaf_far = far[:box_dom]
    parent_locals = far[box_dom:]
    downward = jnp.einsum(
        "qd,cds->qcs", parent_locals, upward_translation_table, precision=top
    ).reshape(box_dom, coeffs)
    domain_local = leaf_far + downward
    box_locals = lax.dynamic_slice_in_dim(domain_local, me * leaves, leaves, axis=0)
    block_locals = jnp.dot(box_hot, domain_local, precision=top)
    coulomb = block_coulomb(bra_table, ket_table, block_locals)
    return (coulomb, box_locals)


def solution(mesh):
    placed = (
        P(("space", "blk"), None, None),
        P(("space", "blk"), None, None),
        P(("space", "blk"), None, None),
        P(("space", "blk")),
        P(("space", "blk"), None),
        P(("space", "blk"), None),
        P(("space", "blk"), None),
        P(("space", "blk"), None),
        P(),
        P(),
    )
    return jax.shard_map(
        shards,
        mesh=mesh,
        in_specs=placed,
        out_specs=(P(("space", "blk"), None, None), P(("space", "blk"), None)),
        check_vma=False,
    )
```

```python
import jax
import jax.numpy as jnp
from jax import lax
from jax.experimental import pallas as pl
from jax.experimental.pallas import tpu as pltpu
from jax.sharding import PartitionSpec as P

def tile_of(blocks, most=48):
    for tile in range(most, 7, -8):
        if blocks % tile == 0:
            return tile
    return blocks


def moments_kernel(dens_ref, bra_ref, ket_ref, out_ref):
    for j in range(out_ref.shape[0]):
        mixed = jnp.dot(dens_ref[j], ket_ref[j], preferred_element_type=jnp.float32)
        out_ref[pl.ds(j, 1), :] = jnp.sum(
            bra_ref[j].astype(jnp.float32) * mixed, axis=0, keepdims=True
        )


def block_moments(density, bra_table, ket_table):
    blocks, rows, cols = density.shape
    coeffs = bra_table.shape[2]
    tile = tile_of(blocks)
    return pl.pallas_call(
        moments_kernel,
        out_shape=jax.ShapeDtypeStruct((blocks, coeffs), jnp.float32),
        grid=(blocks // tile,),
        in_specs=[
            pl.BlockSpec((tile, rows, cols), lambda i: (i, 0, 0)),
            pl.BlockSpec((tile, rows, coeffs), lambda i: (i, 0, 0)),
            pl.BlockSpec((tile, cols, coeffs), lambda i: (i, 0, 0)),
        ],
        out_specs=pl.BlockSpec((tile, coeffs), lambda i: (i, 0)),
        cost_estimate=pl.CostEstimate(
            flops=2 * blocks * rows * cols * coeffs,
            transcendentals=0,
            bytes_accessed=2 * blocks * (rows * cols + 2 * rows * coeffs) + 4 * blocks * coeffs,
        ),
    )(density, bra_table, ket_table)


def coulomb_kernel(bra_ref, ket_ref, local_ref, out_ref):
    for j in range(out_ref.shape[0]):
        scaled = (bra_ref[j].astype(jnp.float32) * local_ref[pl.ds(j, 1), :]).astype(jnp.bfloat16)
        out_ref[j] = lax.dot_general(
            scaled, ket_ref[j], (((1,), (1,)), ((), ())), preferred_element_type=jnp.float32
        ).astype(jnp.bfloat16)


def block_coulomb(bra_table, ket_table, block_locals):
    blocks, rows, coeffs = bra_table.shape
    cols = ket_table.shape[1]
    tile = tile_of(blocks)
    return pl.pallas_call(
        coulomb_kernel,
        out_shape=jax.ShapeDtypeStruct((blocks, rows, cols), jnp.bfloat16),
        grid=(blocks // tile,),
        in_specs=[
            pl.BlockSpec((tile, rows, coeffs), lambda i: (i, 0, 0)),
            pl.BlockSpec((tile, cols, coeffs), lambda i: (i, 0, 0)),
            pl.BlockSpec((tile, coeffs), lambda i: (i, 0)),
        ],
        out_specs=pl.BlockSpec((tile, rows, cols), lambda i: (i, 0, 0)),
        cost_estimate=pl.CostEstimate(
            flops=2 * blocks * rows * cols * coeffs,
            transcendentals=0,
            bytes_accessed=2 * blocks * (rows * cols + 2 * rows * coeffs) + 4 * blocks * coeffs,
        ),
    )(bra_table, ket_table, block_locals)


def exchange(x, axis, mask):
    count = lax.axis_size(axis)
    return lax.ppermute(x, axis, [(i, i ^ mask) for i in range(count)])


def butterfly_sum(x, axis):
    count = lax.axis_size(axis)
    mask = 1
    while mask < count:
        x = x + exchange(x, axis, mask)
        mask *= 2
    return x


def butterfly_gather(x, axis):
    count = lax.axis_size(axis)
    me = lax.axis_index(axis)
    mask = 1
    while mask < count:
        other = exchange(x, axis, mask)
        low = (me // mask) % 2 == 0
        x = jnp.where(low, jnp.concatenate([x, other], 0), jnp.concatenate([other, x], 0))
        mask *= 2
    return x


def shards(
    density,
    bra_table,
    ket_table,
    box_of_block,
    leaf_src,
    leaf_type,
    coarse_src,
    coarse_type,
    translation,
    upward_translation_table,
):
    top = lax.Precision.HIGH
    n_blk = lax.axis_size("blk")
    n_space = lax.axis_size("space")
    me = lax.axis_index("blk")
    here = lax.axis_index("space")
    leaves = leaf_src.shape[0]
    box_dom = leaves * n_blk
    n_types = translation.shape[0]
    coeffs = translation.shape[1]

    core = me % 2
    core0 = core == 0
    half = box_dom // 2

    lists = jnp.concatenate([leaf_src, leaf_type, coarse_src, coarse_type], axis=0)
    flat = lists.size
    table = jnp.zeros((n_blk, flat), jnp.float32)
    table = lax.dynamic_update_index_in_dim(table, lists.reshape(flat).astype(jnp.float32), me, 0)
    table_rows = 2 * -(-n_blk * flat // (2 * coeffs))
    table = jnp.pad(table.reshape(-1), (0, table_rows * coeffs - n_blk * flat))
    table = table.reshape(table_rows, coeffs)

    moments = block_moments(density, bra_table, ket_table)
    box_hot = (box_of_block[:, None] == jnp.arange(box_dom, dtype=jnp.int32)[None, :]).astype(
        jnp.float32
    )
    partial_moments = lax.dot_general(
        box_hot, moments, (((0,), (0,)), ((), ())), precision=top
    )
    first = jnp.concatenate([partial_moments[:half], table], axis=0)
    second = jnp.concatenate([partial_moments[half:], table], axis=0)
    mine = jnp.where(core0, first, second)
    summed = mine + exchange(jnp.where(core0, second, first), "blk", 1)
    mask = 2
    while mask < n_blk:
        summed = summed + exchange(summed, "blk", mask)
        mask *= 2
    leaf_half = summed[:half]
    table = summed[half:]

    parent_half = jnp.einsum(
        "qce,cde->qd", leaf_half.reshape(-1, 8, coeffs), upward_translation_table, precision=top
    )
    p_half = parent_half.shape[0]
    parents = parent_half
    carried = leaf_half
    delivered = []
    mask = 1
    while mask < n_space:
        got = exchange(jnp.concatenate([carried, parents], axis=0), "space", mask)
        carried = got[:half]
        delivered.append(carried)
        parents = jnp.concatenate([parents, got[half:]], axis=0)
        mask *= 2

    def neighbour(step):
        other = here + step
        pick = jnp.zeros_like(leaf_half)
        for r, block in enumerate(delivered):
            pick = jnp.where((here ^ other) == 2 ** (r + 1) - 1, block, pick)
        inside = (other >= 0) & (other < n_space)
        return jnp.where(inside, pick, 0.0)

    window = jnp.concatenate([neighbour(-1), leaf_half, neighbour(1)], axis=0)
    rows_held = (
        jnp.arange(3)[:, None] * box_dom + core * half + jnp.arange(half)[None, :]
    ).reshape(-1)
    slots = parents.shape[0] // p_half
    parents_held = (
        jnp.arange(slots)[:, None] * n_blk + core * p_half + jnp.arange(p_half)[None, :]
    ).reshape(-1)
    table = table.reshape(-1)[: n_blk * flat].reshape((n_blk,) + lists.shape)
    table = table.astype(jnp.int32)
    dom_src = table[:, :leaves].reshape(box_dom, -1)
    dom_type = table[:, leaves : 2 * leaves].reshape(box_dom, -1)
    dom_csrc = table[:, 2 * leaves]
    dom_ctype = table[:, 2 * leaves + 1]
    dom_csrc = (dom_csrc // n_blk ^ here) * n_blk + dom_csrc % n_blk

    src_hot = (dom_src[..., None] == rows_held).astype(jnp.bfloat16)
    type_hot = (dom_type[..., None] == jnp.arange(n_types, dtype=jnp.int32)).astype(jnp.bfloat16)
    counts = jnp.einsum("blt,blj->btj", type_hot, src_hot, preferred_element_type=jnp.float32)
    gathered = jnp.einsum("btj,jk->btk", counts, window, precision=top)
    csrc_hot = (dom_csrc[..., None] == parents_held).astype(jnp.bfloat16)
    ctype_hot = (dom_ctype[..., None] == jnp.arange(n_types, dtype=jnp.int32)).astype(jnp.bfloat16)
    ccounts = jnp.einsum("pet,peq->ptq", ctype_hot, csrc_hot, preferred_element_type=jnp.float32)
    cgathered = jnp.einsum("ptq,qk->ptk", ccounts, parents, precision=top)
    rows = jnp.concatenate([gathered, cgathered], axis=0)
    far_part = jnp.einsum("btk,tlk->bl", rows, translation, precision=top)
    far = far_part + exchange(far_part, "blk", 1)
    leaf_far = far[:box_dom]
    parent_locals = far[box_dom:]
    downward = jnp.einsum(
        "qd,cds->qcs", parent_locals, upward_translation_table, precision=top
    ).reshape(box_dom, coeffs)
    domain_local = leaf_far + downward
    box_locals = lax.dynamic_slice_in_dim(domain_local, me * leaves, leaves, axis=0)
    block_locals = jnp.dot(box_hot, domain_local, precision=top)
    coulomb = block_coulomb(bra_table, ket_table, block_locals)
    return (coulomb, box_locals)


def solution(mesh):
    placed = (
        P(("space", "blk"), None, None),
        P(("space", "blk"), None, None),
        P(("space", "blk"), None, None),
        P(("space", "blk")),
        P(("space", "blk"), None),
        P(("space", "blk"), None),
        P(("space", "blk"), None),
        P(("space", "blk"), None),
        P(),
        P(),
    )
    return jax.shard_map(
        shards,
        mesh=mesh,
        in_specs=placed,
        out_specs=(P(("space", "blk"), None, None), P(("space", "blk"), None)),
        check_vma=False,
    )
```

```python
import jax
import jax.numpy as jnp
from jax import lax
from jax.experimental import pallas as pl
from jax.experimental.pallas import tpu as pltpu
from jax.sharding import PartitionSpec as P

def tile_of(blocks, most=48):
    for tile in range(most, 7, -8):
        if blocks % tile == 0:
            return tile
    return blocks


def moments_kernel(dens_ref, bra_ref, ket_ref, out_ref):
    for j in range(out_ref.shape[0]):
        mixed = jnp.dot(dens_ref[j], ket_ref[j], preferred_element_type=jnp.float32)
        out_ref[pl.ds(j, 1), :] = jnp.sum(
            bra_ref[j].astype(jnp.float32) * mixed, axis=0, keepdims=True
        )


def block_moments(density, bra_table, ket_table):
    blocks, rows, cols = density.shape
    coeffs = bra_table.shape[2]
    tile = tile_of(blocks)
    return pl.pallas_call(
        moments_kernel,
        out_shape=jax.ShapeDtypeStruct((blocks, coeffs), jnp.float32),
        grid=(blocks // tile,),
        in_specs=[
            pl.BlockSpec((tile, rows, cols), lambda i: (i, 0, 0)),
            pl.BlockSpec((tile, rows, coeffs), lambda i: (i, 0, 0)),
            pl.BlockSpec((tile, cols, coeffs), lambda i: (i, 0, 0)),
        ],
        out_specs=pl.BlockSpec((tile, coeffs), lambda i: (i, 0)),
        cost_estimate=pl.CostEstimate(
            flops=2 * blocks * rows * cols * coeffs,
            transcendentals=0,
            bytes_accessed=2 * blocks * (rows * cols + 2 * rows * coeffs) + 4 * blocks * coeffs,
        ),
    )(density, bra_table, ket_table)


def coulomb_kernel(bra_ref, ket_ref, local_ref, out_ref):
    for j in range(out_ref.shape[0]):
        scaled = (bra_ref[j].astype(jnp.float32) * local_ref[pl.ds(j, 1), :]).astype(jnp.bfloat16)
        out_ref[j] = lax.dot_general(
            scaled, ket_ref[j], (((1,), (1,)), ((), ())), preferred_element_type=jnp.float32
        ).astype(jnp.bfloat16)


def block_coulomb(bra_table, ket_table, block_locals):
    blocks, rows, coeffs = bra_table.shape
    cols = ket_table.shape[1]
    tile = tile_of(blocks)
    return pl.pallas_call(
        coulomb_kernel,
        out_shape=jax.ShapeDtypeStruct((blocks, rows, cols), jnp.bfloat16),
        grid=(blocks // tile,),
        in_specs=[
            pl.BlockSpec((tile, rows, coeffs), lambda i: (i, 0, 0)),
            pl.BlockSpec((tile, cols, coeffs), lambda i: (i, 0, 0)),
            pl.BlockSpec((tile, coeffs), lambda i: (i, 0)),
        ],
        out_specs=pl.BlockSpec((tile, rows, cols), lambda i: (i, 0, 0)),
        cost_estimate=pl.CostEstimate(
            flops=2 * blocks * rows * cols * coeffs,
            transcendentals=0,
            bytes_accessed=2 * blocks * (rows * cols + 2 * rows * coeffs) + 4 * blocks * coeffs,
        ),
    )(bra_table, ket_table, block_locals)


def exchange(x, axis, mask):
    count = lax.axis_size(axis)
    return lax.ppermute(x, axis, [(i, i ^ mask) for i in range(count)])


def butterfly_sum(x, axis):
    count = lax.axis_size(axis)
    mask = 1
    while mask < count:
        x = x + exchange(x, axis, mask)
        mask *= 2
    return x


def butterfly_gather(x, axis):
    count = lax.axis_size(axis)
    me = lax.axis_index(axis)
    mask = 1
    while mask < count:
        other = exchange(x, axis, mask)
        low = (me // mask) % 2 == 0
        x = jnp.where(low, jnp.concatenate([x, other], 0), jnp.concatenate([other, x], 0))
        mask *= 2
    return x


def shards(
    density,
    bra_table,
    ket_table,
    box_of_block,
    leaf_src,
    leaf_type,
    coarse_src,
    coarse_type,
    translation,
    upward_translation_table,
):
    top = lax.Precision.HIGH
    n_blk = lax.axis_size("blk")
    n_space = lax.axis_size("space")
    me = lax.axis_index("blk")
    here = lax.axis_index("space")
    leaves = leaf_src.shape[0]
    box_dom = leaves * n_blk
    n_types = translation.shape[0]
    coeffs = translation.shape[1]

    core = me % 2
    core0 = core == 0
    half = box_dom // 2

    lists = jnp.concatenate([leaf_src, leaf_type, coarse_src, coarse_type], axis=0)
    flat = lists.size
    slot_rows = -(-flat // coeffs)
    slot = jnp.pad(lists.reshape(flat).astype(jnp.float32), (0, slot_rows * coeffs - flat))
    slot = slot.reshape(slot_rows, coeffs)

    moments = block_moments(density, bra_table, ket_table)
    box_hot = (box_of_block[:, None] == jnp.arange(box_dom, dtype=jnp.int32)[None, :]).astype(
        jnp.float32
    )
    partial_moments = lax.dot_general(
        box_hot, moments, (((0,), (0,)), ((), ())), precision=top
    )
    first = partial_moments[:half]
    second = partial_moments[half:]
    got = exchange(jnp.concatenate([jnp.where(core0, second, first), slot], axis=0), "blk", 1)
    summed = jnp.where(core0, first, second) + got[:half]
    gathered_lists = jnp.concatenate([slot, got[half:]], axis=0)
    mask = 2
    while mask < n_blk:
        got = exchange(jnp.concatenate([summed, gathered_lists], axis=0), "blk", mask)
        summed = summed + got[:half]
        gathered_lists = jnp.concatenate([gathered_lists, got[half:]], axis=0)
        mask *= 2
    leaf_half = summed
    base = me - core
    by_slot = gathered_lists.reshape(n_blk, slot_rows * coeffs)
    paired = by_slot.reshape(n_blk // 2, 2, -1)[:, ::-1].reshape(n_blk, -1)
    by_slot = jnp.where(core0, by_slot, paired)

    parent_half = jnp.einsum(
        "qce,cde->qd", leaf_half.reshape(-1, 8, coeffs), upward_translation_table, precision=top
    )
    p_half = parent_half.shape[0]
    parents = parent_half
    carried = leaf_half
    delivered = []
    mask = 1
    while mask < n_space:
        got = exchange(jnp.concatenate([carried, parents], axis=0), "space", mask)
        carried = got[:half]
        delivered.append(carried)
        parents = jnp.concatenate([parents, got[half:]], axis=0)
        mask *= 2

    def neighbour(step):
        other = here + step
        pick = jnp.zeros_like(leaf_half)
        for r, block in enumerate(delivered):
            pick = jnp.where((here ^ other) == 2 ** (r + 1) - 1, block, pick)
        inside = (other >= 0) & (other < n_space)
        return jnp.where(inside, pick, 0.0)

    window = jnp.concatenate([neighbour(-1), leaf_half, neighbour(1)], axis=0)
    rows_held = (
        jnp.arange(3)[:, None] * box_dom + core * half + jnp.arange(half)[None, :]
    ).reshape(-1)
    slots = parents.shape[0] // p_half
    parents_held = (
        jnp.arange(slots)[:, None] * n_blk + core * p_half + jnp.arange(p_half)[None, :]
    ).reshape(-1)
    table = by_slot[:, :flat].reshape((n_blk,) + lists.shape).astype(jnp.int32)
    dom_src = table[:, :leaves].reshape(box_dom, -1)
    dom_type = table[:, leaves : 2 * leaves].reshape(box_dom, -1)
    dom_csrc = table[:, 2 * leaves]
    dom_ctype = table[:, 2 * leaves + 1]
    dom_csrc = (dom_csrc // n_blk ^ here) * n_blk + dom_csrc % n_blk

    src_hot = (dom_src[..., None] == rows_held).astype(jnp.bfloat16)
    type_hot = (dom_type[..., None] == jnp.arange(n_types, dtype=jnp.int32)).astype(jnp.bfloat16)
    counts = jnp.einsum("blt,blj->btj", type_hot, src_hot, preferred_element_type=jnp.float32)
    gathered = jnp.einsum("btj,jk->btk", counts, window, precision=top)
    csrc_hot = (dom_csrc[..., None] == parents_held).astype(jnp.bfloat16)
    ctype_hot = (dom_ctype[..., None] == jnp.arange(n_types, dtype=jnp.int32)).astype(jnp.bfloat16)
    ccounts = jnp.einsum("pet,peq->ptq", ctype_hot, csrc_hot, preferred_element_type=jnp.float32)
    cgathered = jnp.einsum("ptq,qk->ptk", ccounts, parents, precision=top)
    rows = jnp.concatenate([gathered, cgathered], axis=0)
    far_part = jnp.einsum("btk,tlk->bl", rows, translation, precision=top)
    far = far_part + exchange(far_part, "blk", 1)
    leaf_far = far[:box_dom]
    parent_locals = far[box_dom:]
    downward = jnp.einsum(
        "qd,cds->qcs", parent_locals, upward_translation_table, precision=top
    ).reshape(box_dom, coeffs)
    domain_local = leaf_far + downward
    box_locals = lax.dynamic_slice_in_dim(domain_local, core * leaves, leaves, axis=0)
    relabelled = ((box_of_block // leaves) ^ base) * leaves + box_of_block % leaves
    slot_hot = (relabelled[:, None] == jnp.arange(box_dom, dtype=jnp.int32)[None, :]).astype(
        jnp.float32
    )
    block_locals = jnp.dot(slot_hot, domain_local, precision=top)
    coulomb = block_coulomb(bra_table, ket_table, block_locals)
    return (coulomb, box_locals)


def solution(mesh):
    placed = (
        P(("space", "blk"), None, None),
        P(("space", "blk"), None, None),
        P(("space", "blk"), None, None),
        P(("space", "blk")),
        P(("space", "blk"), None),
        P(("space", "blk"), None),
        P(("space", "blk"), None),
        P(("space", "blk"), None),
        P(),
        P(),
    )
    return jax.shard_map(
        shards,
        mesh=mesh,
        in_specs=placed,
        out_specs=(P(("space", "blk"), None, None), P(("space", "blk"), None)),
        check_vma=False,
    )
```

```python
import jax
import jax.numpy as jnp
from jax import lax
from jax.experimental import pallas as pl
from jax.experimental.pallas import tpu as pltpu
from jax.sharding import PartitionSpec as P

def tile_of(blocks, most=48):
    for tile in range(most, 7, -8):
        if blocks % tile == 0:
            return tile
    return blocks


def moments_kernel(dens_ref, bra_ref, ket_ref, out_ref):
    for j in range(out_ref.shape[0]):
        mixed = jnp.dot(dens_ref[j], ket_ref[j], preferred_element_type=jnp.float32)
        out_ref[pl.ds(j, 1), :] = jnp.sum(
            bra_ref[j].astype(jnp.float32) * mixed, axis=0, keepdims=True
        )


def block_moments(density, bra_table, ket_table):
    blocks, rows, cols = density.shape
    coeffs = bra_table.shape[2]
    tile = tile_of(blocks)
    return pl.pallas_call(
        moments_kernel,
        out_shape=jax.ShapeDtypeStruct((blocks, coeffs), jnp.float32),
        grid=(blocks // tile,),
        in_specs=[
            pl.BlockSpec((tile, rows, cols), lambda i: (i, 0, 0)),
            pl.BlockSpec((tile, rows, coeffs), lambda i: (i, 0, 0)),
            pl.BlockSpec((tile, cols, coeffs), lambda i: (i, 0, 0)),
        ],
        out_specs=pl.BlockSpec((tile, coeffs), lambda i: (i, 0)),
        cost_estimate=pl.CostEstimate(
            flops=2 * blocks * rows * cols * coeffs,
            transcendentals=0,
            bytes_accessed=2 * blocks * (rows * cols + 2 * rows * coeffs) + 4 * blocks * coeffs,
        ),
    )(density, bra_table, ket_table)


def coulomb_kernel(bra_ref, ket_ref, local_ref, out_ref):
    for j in range(out_ref.shape[0]):
        scaled = (bra_ref[j].astype(jnp.float32) * local_ref[pl.ds(j, 1), :]).astype(jnp.bfloat16)
        out_ref[j] = lax.dot_general(
            scaled, ket_ref[j], (((1,), (1,)), ((), ())), preferred_element_type=jnp.float32
        ).astype(jnp.bfloat16)


def block_coulomb(bra_table, ket_table, block_locals):
    blocks, rows, coeffs = bra_table.shape
    cols = ket_table.shape[1]
    tile = tile_of(blocks)
    return pl.pallas_call(
        coulomb_kernel,
        out_shape=jax.ShapeDtypeStruct((blocks, rows, cols), jnp.bfloat16),
        grid=(blocks // tile,),
        in_specs=[
            pl.BlockSpec((tile, rows, coeffs), lambda i: (i, 0, 0)),
            pl.BlockSpec((tile, cols, coeffs), lambda i: (i, 0, 0)),
            pl.BlockSpec((tile, coeffs), lambda i: (i, 0)),
        ],
        out_specs=pl.BlockSpec((tile, rows, cols), lambda i: (i, 0, 0)),
        cost_estimate=pl.CostEstimate(
            flops=2 * blocks * rows * cols * coeffs,
            transcendentals=0,
            bytes_accessed=2 * blocks * (rows * cols + 2 * rows * coeffs) + 4 * blocks * coeffs,
        ),
    )(bra_table, ket_table, block_locals)


def exact_left(spec, left, right):
    high = right.astype(jnp.bfloat16)
    low = (right - high.astype(jnp.float32)).astype(jnp.bfloat16)
    left = left.astype(jnp.bfloat16)
    return jnp.einsum(spec, left, high, preferred_element_type=jnp.float32) + jnp.einsum(
        spec, left, low, preferred_element_type=jnp.float32
    )


def exchange(x, axis, mask):
    count = lax.axis_size(axis)
    return lax.ppermute(x, axis, [(i, i ^ mask) for i in range(count)])


def butterfly_sum(x, axis):
    count = lax.axis_size(axis)
    mask = 1
    while mask < count:
        x = x + exchange(x, axis, mask)
        mask *= 2
    return x


def butterfly_gather(x, axis):
    count = lax.axis_size(axis)
    me = lax.axis_index(axis)
    mask = 1
    while mask < count:
        other = exchange(x, axis, mask)
        low = (me // mask) % 2 == 0
        x = jnp.where(low, jnp.concatenate([x, other], 0), jnp.concatenate([other, x], 0))
        mask *= 2
    return x


def shards(
    density,
    bra_table,
    ket_table,
    box_of_block,
    leaf_src,
    leaf_type,
    coarse_src,
    coarse_type,
    translation,
    upward_translation_table,
):
    top = lax.Precision.HIGH
    n_blk = lax.axis_size("blk")
    n_space = lax.axis_size("space")
    me = lax.axis_index("blk")
    here = lax.axis_index("space")
    leaves = leaf_src.shape[0]
    box_dom = leaves * n_blk
    n_types = translation.shape[0]
    coeffs = translation.shape[1]

    core = me % 2
    core0 = core == 0
    half = box_dom // 2

    lists = jnp.concatenate([leaf_src, leaf_type, coarse_src, coarse_type], axis=0)
    flat = lists.size
    slot_rows = -(-flat // coeffs)
    slot = jnp.pad(lists.reshape(flat).astype(jnp.float32), (0, slot_rows * coeffs - flat))
    slot = slot.reshape(slot_rows, coeffs)

    moments = block_moments(density, bra_table, ket_table)
    box_hot = (box_of_block[:, None] == jnp.arange(box_dom, dtype=jnp.int32)[None, :]).astype(
        jnp.float32
    )
    partial_moments = exact_left("bj,bk->jk", box_hot, moments)
    first = partial_moments[:half]
    second = partial_moments[half:]
    got = exchange(jnp.concatenate([jnp.where(core0, second, first), slot], axis=0), "blk", 1)
    summed = jnp.where(core0, first, second) + got[:half]
    gathered_lists = jnp.concatenate([slot, got[half:]], axis=0)
    mask = 2
    while mask < n_blk:
        got = exchange(jnp.concatenate([summed, gathered_lists], axis=0), "blk", mask)
        summed = summed + got[:half]
        gathered_lists = jnp.concatenate([gathered_lists, got[half:]], axis=0)
        mask *= 2
    leaf_half = summed
    base = me - core
    by_slot = gathered_lists.reshape(n_blk, slot_rows * coeffs)
    paired = by_slot.reshape(n_blk // 2, 2, -1)[:, ::-1].reshape(n_blk, -1)
    by_slot = jnp.where(core0, by_slot, paired)

    parent_half = jnp.einsum(
        "qce,cde->qd", leaf_half.reshape(-1, 8, coeffs), upward_translation_table, precision=top
    )
    p_half = parent_half.shape[0]
    parents = parent_half
    carried = leaf_half
    delivered = []
    mask = 1
    while mask < n_space:
        got = exchange(jnp.concatenate([carried, parents], axis=0), "space", mask)
        carried = got[:half]
        delivered.append(carried)
        parents = jnp.concatenate([parents, got[half:]], axis=0)
        mask *= 2

    def neighbour(step):
        other = here + step
        pick = jnp.zeros_like(leaf_half)
        for r, block in enumerate(delivered):
            pick = jnp.where((here ^ other) == 2 ** (r + 1) - 1, block, pick)
        inside = (other >= 0) & (other < n_space)
        return jnp.where(inside, pick, 0.0)

    window = jnp.concatenate([neighbour(-1), leaf_half, neighbour(1)], axis=0)
    rows_held = (
        jnp.arange(3)[:, None] * box_dom + core * half + jnp.arange(half)[None, :]
    ).reshape(-1)
    slots = parents.shape[0] // p_half
    parents_held = (
        jnp.arange(slots)[:, None] * n_blk + core * p_half + jnp.arange(p_half)[None, :]
    ).reshape(-1)
    table = by_slot[:, :flat].reshape((n_blk,) + lists.shape).astype(jnp.int32)
    dom_src = table[:, :leaves].reshape(box_dom, -1)
    dom_type = table[:, leaves : 2 * leaves].reshape(box_dom, -1)
    dom_csrc = table[:, 2 * leaves]
    dom_ctype = table[:, 2 * leaves + 1]
    dom_csrc = (dom_csrc // n_blk ^ here) * n_blk + dom_csrc % n_blk

    src_hot = (dom_src[..., None] == rows_held).astype(jnp.bfloat16)
    type_hot = (dom_type[..., None] == jnp.arange(n_types, dtype=jnp.int32)).astype(jnp.bfloat16)
    counts = jnp.einsum("blt,blj->btj", type_hot, src_hot, preferred_element_type=jnp.float32)
    gathered = exact_left("btj,jk->btk", counts, window)
    csrc_hot = (dom_csrc[..., None] == parents_held).astype(jnp.bfloat16)
    ctype_hot = (dom_ctype[..., None] == jnp.arange(n_types, dtype=jnp.int32)).astype(jnp.bfloat16)
    ccounts = jnp.einsum("pet,peq->ptq", ctype_hot, csrc_hot, preferred_element_type=jnp.float32)
    cgathered = exact_left("ptq,qk->ptk", ccounts, parents)
    rows = jnp.concatenate([gathered, cgathered], axis=0)
    far_part = jnp.einsum("btk,tlk->bl", rows, translation, precision=top)
    far = far_part + exchange(far_part, "blk", 1)
    leaf_far = far[:box_dom]
    parent_locals = far[box_dom:]
    downward = jnp.einsum(
        "qd,cds->qcs", parent_locals, upward_translation_table, precision=top
    ).reshape(box_dom, coeffs)
    domain_local = leaf_far + downward
    box_locals = lax.dynamic_slice_in_dim(domain_local, core * leaves, leaves, axis=0)
    relabelled = ((box_of_block // leaves) ^ base) * leaves + box_of_block % leaves
    slot_hot = (relabelled[:, None] == jnp.arange(box_dom, dtype=jnp.int32)[None, :]).astype(
        jnp.float32
    )
    block_locals = exact_left("bj,jk->bk", slot_hot, domain_local)
    coulomb = block_coulomb(bra_table, ket_table, block_locals)
    return (coulomb, box_locals)


def solution(mesh):
    placed = (
        P(("space", "blk"), None, None),
        P(("space", "blk"), None, None),
        P(("space", "blk"), None, None),
        P(("space", "blk")),
        P(("space", "blk"), None),
        P(("space", "blk"), None),
        P(("space", "blk"), None),
        P(("space", "blk"), None),
        P(),
        P(),
    )
    return jax.shard_map(
        shards,
        mesh=mesh,
        in_specs=placed,
        out_specs=(P(("space", "blk"), None, None), P(("space", "blk"), None)),
        check_vma=False,
    )
```

```python
import jax
import jax.numpy as jnp
from jax import lax
from jax.experimental import pallas as pl
from jax.experimental.pallas import tpu as pltpu
from jax.sharding import PartitionSpec as P

def tile_of(blocks, most=48):
    for tile in range(most, 7, -8):
        if blocks % tile == 0:
            return tile
    return blocks


def moments_kernel(dens_ref, bra_ref, ket_ref, out_ref):
    for j in range(out_ref.shape[0]):
        mixed = jnp.dot(dens_ref[j], ket_ref[j], preferred_element_type=jnp.float32)
        out_ref[pl.ds(j, 1), :] = jnp.sum(
            bra_ref[j].astype(jnp.float32) * mixed, axis=0, keepdims=True
        )


def block_moments(density, bra_table, ket_table):
    blocks, rows, cols = density.shape
    coeffs = bra_table.shape[2]
    tile = tile_of(blocks)
    return pl.pallas_call(
        moments_kernel,
        out_shape=jax.ShapeDtypeStruct((blocks, coeffs), jnp.float32),
        grid=(blocks // tile,),
        in_specs=[
            pl.BlockSpec((tile, rows, cols), lambda i: (i, 0, 0)),
            pl.BlockSpec((tile, rows, coeffs), lambda i: (i, 0, 0)),
            pl.BlockSpec((tile, cols, coeffs), lambda i: (i, 0, 0)),
        ],
        out_specs=pl.BlockSpec((tile, coeffs), lambda i: (i, 0)),
        cost_estimate=pl.CostEstimate(
            flops=2 * blocks * rows * cols * coeffs,
            transcendentals=0,
            bytes_accessed=2 * blocks * (rows * cols + 2 * rows * coeffs) + 4 * blocks * coeffs,
        ),
    )(density, bra_table, ket_table)


def coulomb_kernel(ids_ref, bra_ref, ket_ref, local_ref, out_ref):
    tile = out_ref.shape[0]
    first = pl.program_id(0) * tile
    for j in range(tile):
        local = local_ref[pl.ds(ids_ref[first + j], 1), :]
        scaled = (bra_ref[j].astype(jnp.float32) * local).astype(jnp.bfloat16)
        out_ref[j] = lax.dot_general(
            scaled, ket_ref[j], (((1,), (1,)), ((), ())), preferred_element_type=jnp.float32
        ).astype(jnp.bfloat16)


def block_coulomb(bra_table, ket_table, domain_local, box_ids):
    blocks, rows, coeffs = bra_table.shape
    cols = ket_table.shape[1]
    boxes = domain_local.shape[0]
    tile = tile_of(blocks)
    return pl.pallas_call(
        coulomb_kernel,
        out_shape=jax.ShapeDtypeStruct((blocks, rows, cols), jnp.bfloat16),
        grid_spec=pltpu.PrefetchScalarGridSpec(
            num_scalar_prefetch=1,
            grid=(blocks // tile,),
            in_specs=[
                pl.BlockSpec((tile, rows, coeffs), lambda i, ids: (i, 0, 0)),
                pl.BlockSpec((tile, cols, coeffs), lambda i, ids: (i, 0, 0)),
                pl.BlockSpec((boxes, coeffs), lambda i, ids: (0, 0)),
            ],
            out_specs=pl.BlockSpec((tile, rows, cols), lambda i, ids: (i, 0, 0)),
        ),
        cost_estimate=pl.CostEstimate(
            flops=2 * blocks * rows * cols * coeffs,
            transcendentals=0,
            bytes_accessed=2 * blocks * (rows * cols + 2 * rows * coeffs) + 4 * boxes * coeffs,
        ),
    )(box_ids, bra_table, ket_table, domain_local)


def exchange(x, axis, mask):
    count = lax.axis_size(axis)
    return lax.ppermute(x, axis, [(i, i ^ mask) for i in range(count)])


def butterfly_sum(x, axis):
    count = lax.axis_size(axis)
    mask = 1
    while mask < count:
        x = x + exchange(x, axis, mask)
        mask *= 2
    return x


def butterfly_gather(x, axis):
    count = lax.axis_size(axis)
    me = lax.axis_index(axis)
    mask = 1
    while mask < count:
        other = exchange(x, axis, mask)
        low = (me // mask) % 2 == 0
        x = jnp.where(low, jnp.concatenate([x, other], 0), jnp.concatenate([other, x], 0))
        mask *= 2
    return x


def shards(
    density,
    bra_table,
    ket_table,
    box_of_block,
    leaf_src,
    leaf_type,
    coarse_src,
    coarse_type,
    translation,
    upward_translation_table,
):
    top = lax.Precision.HIGH
    n_blk = lax.axis_size("blk")
    n_space = lax.axis_size("space")
    me = lax.axis_index("blk")
    here = lax.axis_index("space")
    leaves = leaf_src.shape[0]
    box_dom = leaves * n_blk
    n_types = translation.shape[0]
    coeffs = translation.shape[1]

    core = me % 2
    core0 = core == 0
    half = box_dom // 2

    lists = jnp.concatenate([leaf_src, leaf_type, coarse_src, coarse_type], axis=0)
    flat = lists.size
    slot_rows = -(-flat // coeffs)
    slot = jnp.pad(lists.reshape(flat).astype(jnp.float32), (0, slot_rows * coeffs - flat))
    slot = slot.reshape(slot_rows, coeffs)

    moments = block_moments(density, bra_table, ket_table)
    box_hot = (box_of_block[:, None] == jnp.arange(box_dom, dtype=jnp.int32)[None, :]).astype(
        jnp.float32
    )
    partial_moments = lax.dot_general(
        box_hot, moments, (((0,), (0,)), ((), ())), precision=top
    )
    first = partial_moments[:half]
    second = partial_moments[half:]
    got = exchange(jnp.concatenate([jnp.where(core0, second, first), slot], axis=0), "blk", 1)
    summed = jnp.where(core0, first, second) + got[:half]
    gathered_lists = jnp.concatenate([slot, got[half:]], axis=0)
    mask = 2
    while mask < n_blk:
        got = exchange(jnp.concatenate([summed, gathered_lists], axis=0), "blk", mask)
        summed = summed + got[:half]
        gathered_lists = jnp.concatenate([gathered_lists, got[half:]], axis=0)
        mask *= 2
    leaf_half = summed
    base = me - core
    by_slot = gathered_lists.reshape(n_blk, slot_rows * coeffs)
    paired = by_slot.reshape(n_blk // 2, 2, -1)[:, ::-1].reshape(n_blk, -1)
    by_slot = jnp.where(core0, by_slot, paired)

    parent_half = jnp.einsum(
        "qce,cde->qd", leaf_half.reshape(-1, 8, coeffs), upward_translation_table, precision=top
    )
    p_half = parent_half.shape[0]
    parents = parent_half
    carried = leaf_half
    delivered = []
    mask = 1
    while mask < n_space:
        got = exchange(jnp.concatenate([carried, parents], axis=0), "space", mask)
        carried = got[:half]
        delivered.append(carried)
        parents = jnp.concatenate([parents, got[half:]], axis=0)
        mask *= 2

    def neighbour(step):
        other = here + step
        pick = jnp.zeros_like(leaf_half)
        for r, block in enumerate(delivered):
            pick = jnp.where((here ^ other) == 2 ** (r + 1) - 1, block, pick)
        inside = (other >= 0) & (other < n_space)
        return jnp.where(inside, pick, 0.0)

    window = jnp.concatenate([neighbour(-1), leaf_half, neighbour(1)], axis=0)
    rows_held = (
        jnp.arange(3)[:, None] * box_dom + core * half + jnp.arange(half)[None, :]
    ).reshape(-1)
    slots = parents.shape[0] // p_half
    parents_held = (
        jnp.arange(slots)[:, None] * n_blk + core * p_half + jnp.arange(p_half)[None, :]
    ).reshape(-1)
    table = by_slot[:, :flat].reshape((n_blk,) + lists.shape).astype(jnp.int32)
    dom_src = table[:, :leaves].reshape(box_dom, -1)
    dom_type = table[:, leaves : 2 * leaves].reshape(box_dom, -1)
    dom_csrc = table[:, 2 * leaves]
    dom_ctype = table[:, 2 * leaves + 1]
    dom_csrc = (dom_csrc // n_blk ^ here) * n_blk + dom_csrc % n_blk

    src_hot = (dom_src[..., None] == rows_held).astype(jnp.bfloat16)
    type_hot = (dom_type[..., None] == jnp.arange(n_types, dtype=jnp.int32)).astype(jnp.bfloat16)
    counts = jnp.einsum("blt,blj->btj", type_hot, src_hot, preferred_element_type=jnp.float32)
    gathered = jnp.einsum("btj,jk->btk", counts, window, precision=top)
    csrc_hot = (dom_csrc[..., None] == parents_held).astype(jnp.bfloat16)
    ctype_hot = (dom_ctype[..., None] == jnp.arange(n_types, dtype=jnp.int32)).astype(jnp.bfloat16)
    ccounts = jnp.einsum("pet,peq->ptq", ctype_hot, csrc_hot, preferred_element_type=jnp.float32)
    cgathered = jnp.einsum("ptq,qk->ptk", ccounts, parents, precision=top)
    rows = jnp.concatenate([gathered, cgathered], axis=0)
    far_part = jnp.einsum("btk,tlk->bl", rows, translation, precision=top)
    far = far_part + exchange(far_part, "blk", 1)
    leaf_far = far[:box_dom]
    parent_locals = far[box_dom:]
    downward = jnp.einsum(
        "qd,cds->qcs", parent_locals, upward_translation_table, precision=top
    ).reshape(box_dom, coeffs)
    domain_local = leaf_far + downward
    box_locals = lax.dynamic_slice_in_dim(domain_local, core * leaves, leaves, axis=0)
    relabelled = ((box_of_block // leaves) ^ base) * leaves + box_of_block % leaves
    coulomb = block_coulomb(bra_table, ket_table, domain_local, relabelled)
    return (coulomb, box_locals)


def solution(mesh):
    placed = (
        P(("space", "blk"), None, None),
        P(("space", "blk"), None, None),
        P(("space", "blk"), None, None),
        P(("space", "blk")),
        P(("space", "blk"), None),
        P(("space", "blk"), None),
        P(("space", "blk"), None),
        P(("space", "blk"), None),
        P(),
        P(),
    )
    return jax.shard_map(
        shards,
        mesh=mesh,
        in_specs=placed,
        out_specs=(P(("space", "blk"), None, None), P(("space", "blk"), None)),
        check_vma=False,
    )
```

```python
import functools

import jax
import jax.numpy as jnp
from jax import lax
from jax.experimental import pallas as pl
from jax.experimental.pallas import tpu as pltpu
from jax.sharding import PartitionSpec as P

def tile_of(blocks, most=48):
    for tile in range(most, 7, -8):
        if blocks % tile == 0:
            return tile
    return blocks


def moments_kernel(dens_ref, bra_ref, ket_ref, out_ref):
    for j in range(out_ref.shape[0]):
        mixed = jnp.dot(dens_ref[j], ket_ref[j], preferred_element_type=jnp.float32)
        out_ref[pl.ds(j, 1), :] = jnp.sum(
            bra_ref[j].astype(jnp.float32) * mixed, axis=0, keepdims=True
        )


def block_moments(density, bra_table, ket_table):
    blocks, rows, cols = density.shape
    coeffs = bra_table.shape[2]
    tile = tile_of(blocks)
    return pl.pallas_call(
        moments_kernel,
        out_shape=jax.ShapeDtypeStruct((blocks, coeffs), jnp.float32),
        grid=(blocks // tile,),
        in_specs=[
            pl.BlockSpec((tile, rows, cols), lambda i: (i, 0, 0)),
            pl.BlockSpec((tile, rows, coeffs), lambda i: (i, 0, 0)),
            pl.BlockSpec((tile, cols, coeffs), lambda i: (i, 0, 0)),
        ],
        out_specs=pl.BlockSpec((tile, coeffs), lambda i: (i, 0)),
        cost_estimate=pl.CostEstimate(
            flops=2 * blocks * rows * cols * coeffs,
            transcendentals=0,
            bytes_accessed=2 * blocks * (rows * cols + 2 * rows * coeffs) + 4 * blocks * coeffs,
        ),
    )(density, bra_table, ket_table)


def coulomb_kernel(leaves, ids_ref, base_ref, bra_ref, ket_ref, local_ref, out_ref):
    tile = out_ref.shape[0]
    first = pl.program_id(0) * tile
    base = base_ref[0]
    for j in range(tile):
        box = ids_ref[first + j]
        row = ((box // leaves) ^ base) * leaves + box % leaves
        local = local_ref[pl.ds(row, 1), :]
        scaled = (bra_ref[j].astype(jnp.float32) * local).astype(jnp.bfloat16)
        out_ref[j] = lax.dot_general(
            scaled, ket_ref[j], (((1,), (1,)), ((), ())), preferred_element_type=jnp.float32
        ).astype(jnp.bfloat16)


def block_coulomb(bra_table, ket_table, domain_local, box_ids, base, leaves):
    blocks, rows, coeffs = bra_table.shape
    cols = ket_table.shape[1]
    boxes = domain_local.shape[0]
    tile = tile_of(blocks)
    return pl.pallas_call(
        functools.partial(coulomb_kernel, leaves),
        out_shape=jax.ShapeDtypeStruct((blocks, rows, cols), jnp.bfloat16),
        grid_spec=pltpu.PrefetchScalarGridSpec(
            num_scalar_prefetch=2,
            grid=(blocks // tile,),
            in_specs=[
                pl.BlockSpec((tile, rows, coeffs), lambda i, ids, base: (i, 0, 0)),
                pl.BlockSpec((tile, cols, coeffs), lambda i, ids, base: (i, 0, 0)),
                pl.BlockSpec((boxes, coeffs), lambda i, ids, base: (0, 0)),
            ],
            out_specs=pl.BlockSpec((tile, rows, cols), lambda i, ids, base: (i, 0, 0)),
        ),
        cost_estimate=pl.CostEstimate(
            flops=2 * blocks * rows * cols * coeffs,
            transcendentals=0,
            bytes_accessed=2 * blocks * (rows * cols + 2 * rows * coeffs) + 4 * boxes * coeffs,
        ),
    )(box_ids, base, bra_table, ket_table, domain_local)


def exchange(x, axis, mask):
    count = lax.axis_size(axis)
    return lax.ppermute(x, axis, [(i, i ^ mask) for i in range(count)])


def butterfly_sum(x, axis):
    count = lax.axis_size(axis)
    mask = 1
    while mask < count:
        x = x + exchange(x, axis, mask)
        mask *= 2
    return x


def butterfly_gather(x, axis):
    count = lax.axis_size(axis)
    me = lax.axis_index(axis)
    mask = 1
    while mask < count:
        other = exchange(x, axis, mask)
        low = (me // mask) % 2 == 0
        x = jnp.where(low, jnp.concatenate([x, other], 0), jnp.concatenate([other, x], 0))
        mask *= 2
    return x


def shards(
    density,
    bra_table,
    ket_table,
    box_of_block,
    leaf_src,
    leaf_type,
    coarse_src,
    coarse_type,
    translation,
    upward_translation_table,
):
    top = lax.Precision.HIGH
    n_blk = lax.axis_size("blk")
    n_space = lax.axis_size("space")
    me = lax.axis_index("blk")
    here = lax.axis_index("space")
    leaves = leaf_src.shape[0]
    box_dom = leaves * n_blk
    n_types = translation.shape[0]
    coeffs = translation.shape[1]

    core = me % 2
    core0 = core == 0
    half = box_dom // 2

    lists = jnp.concatenate([leaf_src, leaf_type, coarse_src, coarse_type], axis=0)
    flat = lists.size
    slot_rows = -(-flat // coeffs)
    slot = jnp.pad(lists.reshape(flat).astype(jnp.float32), (0, slot_rows * coeffs - flat))
    slot = slot.reshape(slot_rows, coeffs)

    moments = block_moments(density, bra_table, ket_table)
    box_hot = (box_of_block[:, None] == jnp.arange(box_dom, dtype=jnp.int32)[None, :]).astype(
        jnp.float32
    )
    partial_moments = lax.dot_general(
        box_hot, moments, (((0,), (0,)), ((), ())), precision=top
    )
    first = partial_moments[:half]
    second = partial_moments[half:]
    got = exchange(jnp.concatenate([jnp.where(core0, second, first), slot], axis=0), "blk", 1)
    summed = jnp.where(core0, first, second) + got[:half]
    gathered_lists = jnp.concatenate([slot, got[half:]], axis=0)
    mask = 2
    while mask < n_blk:
        got = exchange(jnp.concatenate([summed, gathered_lists], axis=0), "blk", mask)
        summed = summed + got[:half]
        gathered_lists = jnp.concatenate([gathered_lists, got[half:]], axis=0)
        mask *= 2
    leaf_half = summed
    base = me - core
    by_slot = gathered_lists.reshape(n_blk, slot_rows * coeffs)
    paired = by_slot.reshape(n_blk // 2, 2, -1)[:, ::-1].reshape(n_blk, -1)
    by_slot = jnp.where(core0, by_slot, paired)

    parent_half = jnp.einsum(
        "qce,cde->qd", leaf_half.reshape(-1, 8, coeffs), upward_translation_table, precision=top
    )
    p_half = parent_half.shape[0]
    parents = parent_half
    carried = leaf_half
    delivered = []
    mask = 1
    while mask < n_space:
        got = exchange(jnp.concatenate([carried, parents], axis=0), "space", mask)
        carried = got[:half]
        delivered.append(carried)
        parents = jnp.concatenate([parents, got[half:]], axis=0)
        mask *= 2

    def neighbour(step):
        other = here + step
        pick = jnp.zeros_like(leaf_half)
        for r, block in enumerate(delivered):
            pick = jnp.where((here ^ other) == 2 ** (r + 1) - 1, block, pick)
        inside = (other >= 0) & (other < n_space)
        return jnp.where(inside, pick, 0.0)

    window = jnp.concatenate([neighbour(-1), leaf_half, neighbour(1)], axis=0)
    rows_held = (
        jnp.arange(3)[:, None] * box_dom + core * half + jnp.arange(half)[None, :]
    ).reshape(-1)
    slots = parents.shape[0] // p_half
    parents_held = (
        jnp.arange(slots)[:, None] * n_blk + core * p_half + jnp.arange(p_half)[None, :]
    ).reshape(-1)
    table = by_slot[:, :flat].reshape((n_blk,) + lists.shape).astype(jnp.int32)
    dom_src = table[:, :leaves].reshape(box_dom, -1)
    dom_type = table[:, leaves : 2 * leaves].reshape(box_dom, -1)
    dom_csrc = table[:, 2 * leaves]
    dom_ctype = table[:, 2 * leaves + 1]
    dom_csrc = (dom_csrc // n_blk ^ here) * n_blk + dom_csrc % n_blk

    src_hot = (dom_src[..., None] == rows_held).astype(jnp.bfloat16)
    type_hot = (dom_type[..., None] == jnp.arange(n_types, dtype=jnp.int32)).astype(jnp.bfloat16)
    counts = jnp.einsum("blt,blj->btj", type_hot, src_hot, preferred_element_type=jnp.float32)
    gathered = jnp.einsum("btj,jk->btk", counts, window, precision=top)
    csrc_hot = (dom_csrc[..., None] == parents_held).astype(jnp.bfloat16)
    ctype_hot = (dom_ctype[..., None] == jnp.arange(n_types, dtype=jnp.int32)).astype(jnp.bfloat16)
    ccounts = jnp.einsum("pet,peq->ptq", ctype_hot, csrc_hot, preferred_element_type=jnp.float32)
    cgathered = jnp.einsum("ptq,qk->ptk", ccounts, parents, precision=top)
    rows = jnp.concatenate([gathered, cgathered], axis=0)
    far_part = jnp.einsum("btk,tlk->bl", rows, translation, precision=top)
    far = far_part + exchange(far_part, "blk", 1)
    leaf_far = far[:box_dom]
    parent_locals = far[box_dom:]
    downward = jnp.einsum(
        "qd,cds->qcs", parent_locals, upward_translation_table, precision=top
    ).reshape(box_dom, coeffs)
    domain_local = leaf_far + downward
    box_locals = lax.dynamic_slice_in_dim(domain_local, core * leaves, leaves, axis=0)
    coulomb = block_coulomb(
        bra_table, ket_table, domain_local, box_of_block, base.reshape(1).astype(jnp.int32), leaves
    )
    return (coulomb, box_locals)


def solution(mesh):
    placed = (
        P(("space", "blk"), None, None),
        P(("space", "blk"), None, None),
        P(("space", "blk"), None, None),
        P(("space", "blk")),
        P(("space", "blk"), None),
        P(("space", "blk"), None),
        P(("space", "blk"), None),
        P(("space", "blk"), None),
        P(),
        P(),
    )
    return jax.shard_map(
        shards,
        mesh=mesh,
        in_specs=placed,
        out_specs=(P(("space", "blk"), None, None), P(("space", "blk"), None)),
        check_vma=False,
    )
```

```python
import jax
import jax.numpy as jnp
from jax import lax
from jax.experimental import pallas as pl
from jax.experimental.pallas import tpu as pltpu
from jax.sharding import PartitionSpec as P

def tile_of(blocks, most=48):
    for tile in range(most, 7, -8):
        if blocks % tile == 0:
            return tile
    return blocks


def moments_kernel(dens_ref, bra_ref, ket_ref, out_ref):
    for j in range(out_ref.shape[0]):
        mixed = jnp.dot(dens_ref[j], ket_ref[j], preferred_element_type=jnp.float32)
        out_ref[pl.ds(j, 1), :] = jnp.sum(
            bra_ref[j].astype(jnp.float32) * mixed, axis=0, keepdims=True
        )


def block_moments(density, bra_table, ket_table):
    blocks, rows, cols = density.shape
    coeffs = bra_table.shape[2]
    tile = tile_of(blocks)
    return pl.pallas_call(
        moments_kernel,
        out_shape=jax.ShapeDtypeStruct((blocks, coeffs), jnp.float32),
        grid=(blocks // tile,),
        in_specs=[
            pl.BlockSpec((tile, rows, cols), lambda i: (i, 0, 0)),
            pl.BlockSpec((tile, rows, coeffs), lambda i: (i, 0, 0)),
            pl.BlockSpec((tile, cols, coeffs), lambda i: (i, 0, 0)),
        ],
        out_specs=pl.BlockSpec((tile, coeffs), lambda i: (i, 0)),
        cost_estimate=pl.CostEstimate(
            flops=2 * blocks * rows * cols * coeffs,
            transcendentals=0,
            bytes_accessed=2 * blocks * (rows * cols + 2 * rows * coeffs) + 4 * blocks * coeffs,
        ),
    )(density, bra_table, ket_table)


def coulomb_kernel(ids_ref, bra_ref, ket_ref, local_ref, out_ref):
    tile = out_ref.shape[0]
    first = pl.program_id(0) * tile
    for j in range(tile):
        local = local_ref[pl.ds(ids_ref[first + j], 1), :]
        scaled = (bra_ref[j].astype(jnp.float32) * local).astype(jnp.bfloat16)
        out_ref[j] = lax.dot_general(
            scaled, ket_ref[j], (((1,), (1,)), ((), ())), preferred_element_type=jnp.float32
        ).astype(jnp.bfloat16)


def block_coulomb(bra_table, ket_table, domain_local, box_ids):
    blocks, rows, coeffs = bra_table.shape
    cols = ket_table.shape[1]
    boxes = domain_local.shape[0]
    tile = tile_of(blocks)
    return pl.pallas_call(
        coulomb_kernel,
        out_shape=jax.ShapeDtypeStruct((blocks, rows, cols), jnp.bfloat16),
        grid_spec=pltpu.PrefetchScalarGridSpec(
            num_scalar_prefetch=1,
            grid=(blocks // tile,),
            in_specs=[
                pl.BlockSpec((tile, rows, coeffs), lambda i, ids: (i, 0, 0)),
                pl.BlockSpec((tile, cols, coeffs), lambda i, ids: (i, 0, 0)),
                pl.BlockSpec((boxes, coeffs), lambda i, ids: (0, 0)),
            ],
            out_specs=pl.BlockSpec((tile, rows, cols), lambda i, ids: (i, 0, 0)),
        ),
        cost_estimate=pl.CostEstimate(
            flops=2 * blocks * rows * cols * coeffs,
            transcendentals=0,
            bytes_accessed=2 * blocks * (rows * cols + 2 * rows * coeffs) + 4 * boxes * coeffs,
        ),
    )(box_ids, bra_table, ket_table, domain_local)


def exchange(x, axis, mask):
    count = lax.axis_size(axis)
    return lax.ppermute(x, axis, [(i, i ^ mask) for i in range(count)])


def butterfly_sum(x, axis):
    count = lax.axis_size(axis)
    mask = 1
    while mask < count:
        x = x + exchange(x, axis, mask)
        mask *= 2
    return x


def butterfly_gather(x, axis):
    count = lax.axis_size(axis)
    me = lax.axis_index(axis)
    mask = 1
    while mask < count:
        other = exchange(x, axis, mask)
        low = (me // mask) % 2 == 0
        x = jnp.where(low, jnp.concatenate([x, other], 0), jnp.concatenate([other, x], 0))
        mask *= 2
    return x


def shards(
    density,
    bra_table,
    ket_table,
    box_of_block,
    leaf_src,
    leaf_type,
    coarse_src,
    coarse_type,
    translation,
    upward_translation_table,
):
    top = lax.Precision.HIGH
    n_blk = lax.axis_size("blk")
    n_space = lax.axis_size("space")
    me = lax.axis_index("blk")
    here = lax.axis_index("space")
    leaves = leaf_src.shape[0]
    box_dom = leaves * n_blk
    n_types = translation.shape[0]
    coeffs = translation.shape[1]

    core = me % 2
    core0 = core == 0
    half = box_dom // 2

    lists = jnp.concatenate([leaf_src, leaf_type, coarse_src, coarse_type], axis=0)
    flat = lists.size
    slot_rows = -(-flat // coeffs)
    slot = jnp.pad(lists.reshape(flat).astype(jnp.float32), (0, slot_rows * coeffs - flat))
    slot = slot.reshape(slot_rows, coeffs)

    moments = block_moments(density, bra_table, ket_table)
    box_hot = (box_of_block[:, None] == jnp.arange(box_dom, dtype=jnp.int32)[None, :]).astype(
        jnp.float32
    )
    partial_moments = lax.dot_general(
        box_hot, moments, (((0,), (0,)), ((), ())), precision=top
    )
    first = partial_moments[:half]
    second = partial_moments[half:]
    got = exchange(jnp.concatenate([jnp.where(core0, second, first), slot], axis=0), "blk", 1)
    summed = jnp.where(core0, first, second) + got[:half]
    gathered_lists = jnp.concatenate([slot, got[half:]], axis=0)
    mask = 2
    while mask < n_blk:
        got = exchange(jnp.concatenate([summed, gathered_lists], axis=0), "blk", mask)
        summed = summed + got[:half]
        gathered_lists = jnp.concatenate([gathered_lists, got[half:]], axis=0)
        mask *= 2
    leaf_half = summed
    base = me - core
    by_slot = gathered_lists.reshape(n_blk, slot_rows * coeffs)
    paired = by_slot.reshape(n_blk // 2, 2, -1)[:, ::-1].reshape(n_blk, -1)
    by_slot = jnp.where(core0, by_slot, paired)

    parent_half = jnp.einsum(
        "qce,cde->qd", leaf_half.reshape(-1, 8, coeffs), upward_translation_table, precision=top
    )
    p_half = parent_half.shape[0]
    parents = parent_half
    carried = leaf_half
    delivered = []
    mask = 1
    while mask < n_space:
        got = exchange(jnp.concatenate([carried, parents], axis=0), "space", mask)
        carried = got[:half]
        delivered.append(carried)
        parents = jnp.concatenate([parents, got[half:]], axis=0)
        mask *= 2

    def neighbour(step):
        other = here + step
        pick = jnp.zeros_like(leaf_half)
        for r, block in enumerate(delivered):
            pick = jnp.where((here ^ other) == 2 ** (r + 1) - 1, block, pick)
        inside = (other >= 0) & (other < n_space)
        return jnp.where(inside, pick, 0.0)

    window = jnp.concatenate([neighbour(-1), leaf_half, neighbour(1)], axis=0)
    rows_held = (
        jnp.arange(3)[:, None] * box_dom + core * half + jnp.arange(half)[None, :]
    ).reshape(-1)
    slots = parents.shape[0] // p_half
    parents_held = (
        jnp.arange(slots)[:, None] * n_blk + core * p_half + jnp.arange(p_half)[None, :]
    ).reshape(-1)
    table = by_slot[:, :flat].reshape((n_blk,) + lists.shape).astype(jnp.int32)
    dom_src = table[:, :leaves].reshape(box_dom, -1)
    dom_type = table[:, leaves : 2 * leaves].reshape(box_dom, -1)
    dom_csrc = table[:, 2 * leaves]
    dom_ctype = table[:, 2 * leaves + 1]
    dom_csrc = (dom_csrc // n_blk ^ here) * n_blk + dom_csrc % n_blk

    src_hot = (dom_src[..., None] == rows_held).astype(jnp.bfloat16)
    type_hot = (dom_type[..., None] == jnp.arange(n_types, dtype=jnp.int32)).astype(jnp.bfloat16)
    counts = jnp.einsum("blt,blj->btj", type_hot, src_hot, preferred_element_type=jnp.float32)
    gathered = jnp.einsum("btj,jk->btk", counts, window, precision=top)
    csrc_hot = (dom_csrc[..., None] == parents_held).astype(jnp.bfloat16)
    ctype_hot = (dom_ctype[..., None] == jnp.arange(n_types, dtype=jnp.int32)).astype(jnp.bfloat16)
    ccounts = jnp.einsum("pet,peq->ptq", ctype_hot, csrc_hot, preferred_element_type=jnp.float32)
    cgathered = jnp.einsum("ptq,qk->ptk", ccounts, parents, precision=top)
    rows = jnp.concatenate([gathered, cgathered], axis=0)
    far_part = jnp.einsum("btk,tlk->bl", rows, translation, precision=top)
    far = far_part + exchange(far_part, "blk", 1)
    leaf_far = far[:box_dom]
    parent_locals = far[box_dom:]
    downward = jnp.einsum(
        "qd,cds->qcs", parent_locals, upward_translation_table, precision=top
    ).reshape(box_dom, coeffs)
    domain_local = leaf_far + downward
    box_locals = jnp.where(core0, domain_local[:leaves], domain_local[leaves : 2 * leaves])
    relabelled = ((box_of_block // leaves) ^ base) * leaves + box_of_block % leaves
    coulomb = block_coulomb(bra_table, ket_table, domain_local, relabelled)
    return (coulomb, box_locals)


def solution(mesh):
    placed = (
        P(("space", "blk"), None, None),
        P(("space", "blk"), None, None),
        P(("space", "blk"), None, None),
        P(("space", "blk")),
        P(("space", "blk"), None),
        P(("space", "blk"), None),
        P(("space", "blk"), None),
        P(("space", "blk"), None),
        P(),
        P(),
    )
    return jax.shard_map(
        shards,
        mesh=mesh,
        in_specs=placed,
        out_specs=(P(("space", "blk"), None, None), P(("space", "blk"), None)),
        check_vma=False,
    )
```

```python
import jax
import jax.numpy as jnp
from jax import lax
from jax.experimental import pallas as pl
from jax.experimental.pallas import tpu as pltpu
from jax.sharding import PartitionSpec as P

def tile_of(blocks, most=48):
    for tile in range(most, 7, -8):
        if blocks % tile == 0:
            return tile
    return blocks


def moments_kernel(dens_ref, bra_ref, ket_ref, out_ref):
    rows = []
    for j in range(out_ref.shape[0]):
        mixed = jnp.dot(dens_ref[j], ket_ref[j], preferred_element_type=jnp.float32)
        rows.append(jnp.sum(bra_ref[j].astype(jnp.float32) * mixed, axis=0, keepdims=True))
    out_ref[...] = jnp.concatenate(rows, axis=0)


def block_moments(density, bra_table, ket_table):
    blocks, rows, cols = density.shape
    coeffs = bra_table.shape[2]
    tile = tile_of(blocks)
    return pl.pallas_call(
        moments_kernel,
        out_shape=jax.ShapeDtypeStruct((blocks, coeffs), jnp.float32),
        grid=(blocks // tile,),
        in_specs=[
            pl.BlockSpec((tile, rows, cols), lambda i: (i, 0, 0)),
            pl.BlockSpec((tile, rows, coeffs), lambda i: (i, 0, 0)),
            pl.BlockSpec((tile, cols, coeffs), lambda i: (i, 0, 0)),
        ],
        out_specs=pl.BlockSpec((tile, coeffs), lambda i: (i, 0)),
        cost_estimate=pl.CostEstimate(
            flops=2 * blocks * rows * cols * coeffs,
            transcendentals=0,
            bytes_accessed=2 * blocks * (rows * cols + 2 * rows * coeffs) + 4 * blocks * coeffs,
        ),
    )(density, bra_table, ket_table)


def coulomb_kernel(ids_ref, bra_ref, ket_ref, local_ref, out_ref):
    tile = out_ref.shape[0]
    first = pl.program_id(0) * tile
    for j in range(tile):
        local = local_ref[pl.ds(ids_ref[first + j], 1), :]
        scaled = (bra_ref[j].astype(jnp.float32) * local).astype(jnp.bfloat16)
        out_ref[j] = lax.dot_general(
            scaled, ket_ref[j], (((1,), (1,)), ((), ())), preferred_element_type=jnp.float32
        ).astype(jnp.bfloat16)


def block_coulomb(bra_table, ket_table, domain_local, box_ids):
    blocks, rows, coeffs = bra_table.shape
    cols = ket_table.shape[1]
    boxes = domain_local.shape[0]
    tile = tile_of(blocks)
    return pl.pallas_call(
        coulomb_kernel,
        out_shape=jax.ShapeDtypeStruct((blocks, rows, cols), jnp.bfloat16),
        grid_spec=pltpu.PrefetchScalarGridSpec(
            num_scalar_prefetch=1,
            grid=(blocks // tile,),
            in_specs=[
                pl.BlockSpec((tile, rows, coeffs), lambda i, ids: (i, 0, 0)),
                pl.BlockSpec((tile, cols, coeffs), lambda i, ids: (i, 0, 0)),
                pl.BlockSpec((boxes, coeffs), lambda i, ids: (0, 0)),
            ],
            out_specs=pl.BlockSpec((tile, rows, cols), lambda i, ids: (i, 0, 0)),
        ),
        cost_estimate=pl.CostEstimate(
            flops=2 * blocks * rows * cols * coeffs,
            transcendentals=0,
            bytes_accessed=2 * blocks * (rows * cols + 2 * rows * coeffs) + 4 * boxes * coeffs,
        ),
    )(box_ids, bra_table, ket_table, domain_local)


def exchange(x, axis, mask):
    count = lax.axis_size(axis)
    return lax.ppermute(x, axis, [(i, i ^ mask) for i in range(count)])


def butterfly_sum(x, axis):
    count = lax.axis_size(axis)
    mask = 1
    while mask < count:
        x = x + exchange(x, axis, mask)
        mask *= 2
    return x


def butterfly_gather(x, axis):
    count = lax.axis_size(axis)
    me = lax.axis_index(axis)
    mask = 1
    while mask < count:
        other = exchange(x, axis, mask)
        low = (me // mask) % 2 == 0
        x = jnp.where(low, jnp.concatenate([x, other], 0), jnp.concatenate([other, x], 0))
        mask *= 2
    return x


def shards(
    density,
    bra_table,
    ket_table,
    box_of_block,
    leaf_src,
    leaf_type,
    coarse_src,
    coarse_type,
    translation,
    upward_translation_table,
):
    top = lax.Precision.HIGH
    n_blk = lax.axis_size("blk")
    n_space = lax.axis_size("space")
    me = lax.axis_index("blk")
    here = lax.axis_index("space")
    leaves = leaf_src.shape[0]
    box_dom = leaves * n_blk
    n_types = translation.shape[0]
    coeffs = translation.shape[1]

    core = me % 2
    core0 = core == 0
    half = box_dom // 2

    lists = jnp.concatenate([leaf_src, leaf_type, coarse_src, coarse_type], axis=0)
    flat = lists.size
    slot_rows = -(-flat // coeffs)
    slot = jnp.pad(lists.reshape(flat).astype(jnp.float32), (0, slot_rows * coeffs - flat))
    slot = slot.reshape(slot_rows, coeffs)

    moments = block_moments(density, bra_table, ket_table)
    box_hot = (box_of_block[:, None] == jnp.arange(box_dom, dtype=jnp.int32)[None, :]).astype(
        jnp.float32
    )
    partial_moments = lax.dot_general(
        box_hot, moments, (((0,), (0,)), ((), ())), precision=top
    )
    first = partial_moments[:half]
    second = partial_moments[half:]
    got = exchange(jnp.concatenate([jnp.where(core0, second, first), slot], axis=0), "blk", 1)
    summed = jnp.where(core0, first, second) + got[:half]
    gathered_lists = jnp.concatenate([slot, got[half:]], axis=0)
    mask = 2
    while mask < n_blk:
        got = exchange(jnp.concatenate([summed, gathered_lists], axis=0), "blk", mask)
        summed = summed + got[:half]
        gathered_lists = jnp.concatenate([gathered_lists, got[half:]], axis=0)
        mask *= 2
    leaf_half = summed
    base = me - core
    by_slot = gathered_lists.reshape(n_blk, slot_rows * coeffs)
    paired = by_slot.reshape(n_blk // 2, 2, -1)[:, ::-1].reshape(n_blk, -1)
    by_slot = jnp.where(core0, by_slot, paired)

    parent_half = jnp.einsum(
        "qce,cde->qd", leaf_half.reshape(-1, 8, coeffs), upward_translation_table, precision=top
    )
    p_half = parent_half.shape[0]
    parents = parent_half
    carried = leaf_half
    delivered = []
    mask = 1
    while mask < n_space:
        got = exchange(jnp.concatenate([carried, parents], axis=0), "space", mask)
        carried = got[:half]
        delivered.append(carried)
        parents = jnp.concatenate([parents, got[half:]], axis=0)
        mask *= 2

    def neighbour(step):
        other = here + step
        pick = jnp.zeros_like(leaf_half)
        for r, block in enumerate(delivered):
            pick = jnp.where((here ^ other) == 2 ** (r + 1) - 1, block, pick)
        inside = (other >= 0) & (other < n_space)
        return jnp.where(inside, pick, 0.0)

    window = jnp.concatenate([neighbour(-1), leaf_half, neighbour(1)], axis=0)
    rows_held = (
        jnp.arange(3)[:, None] * box_dom + core * half + jnp.arange(half)[None, :]
    ).reshape(-1)
    slots = parents.shape[0] // p_half
    parents_held = (
        jnp.arange(slots)[:, None] * n_blk + core * p_half + jnp.arange(p_half)[None, :]
    ).reshape(-1)
    table = by_slot[:, :flat].reshape((n_blk,) + lists.shape).astype(jnp.int32)
    dom_src = table[:, :leaves].reshape(box_dom, -1)
    dom_type = table[:, leaves : 2 * leaves].reshape(box_dom, -1)
    dom_csrc = table[:, 2 * leaves]
    dom_ctype = table[:, 2 * leaves + 1]
    dom_csrc = (dom_csrc // n_blk ^ here) * n_blk + dom_csrc % n_blk

    src_hot = (dom_src[..., None] == rows_held).astype(jnp.bfloat16)
    type_hot = (dom_type[..., None] == jnp.arange(n_types, dtype=jnp.int32)).astype(jnp.bfloat16)
    counts = jnp.einsum("blt,blj->btj", type_hot, src_hot, preferred_element_type=jnp.float32)
    gathered = jnp.einsum("btj,jk->btk", counts, window, precision=top)
    csrc_hot = (dom_csrc[..., None] == parents_held).astype(jnp.bfloat16)
    ctype_hot = (dom_ctype[..., None] == jnp.arange(n_types, dtype=jnp.int32)).astype(jnp.bfloat16)
    ccounts = jnp.einsum("pet,peq->ptq", ctype_hot, csrc_hot, preferred_element_type=jnp.float32)
    cgathered = jnp.einsum("ptq,qk->ptk", ccounts, parents, precision=top)
    rows = jnp.concatenate([gathered, cgathered], axis=0)
    far_part = jnp.einsum("btk,tlk->bl", rows, translation, precision=top)
    far = far_part + exchange(far_part, "blk", 1)
    leaf_far = far[:box_dom]
    parent_locals = far[box_dom:]
    downward = jnp.einsum(
        "qd,cds->qcs", parent_locals, upward_translation_table, precision=top
    ).reshape(box_dom, coeffs)
    domain_local = leaf_far + downward
    box_locals = lax.dynamic_slice_in_dim(domain_local, core * leaves, leaves, axis=0)
    relabelled = ((box_of_block // leaves) ^ base) * leaves + box_of_block % leaves
    coulomb = block_coulomb(bra_table, ket_table, domain_local, relabelled)
    return (coulomb, box_locals)


def solution(mesh):
    placed = (
        P(("space", "blk"), None, None),
        P(("space", "blk"), None, None),
        P(("space", "blk"), None, None),
        P(("space", "blk")),
        P(("space", "blk"), None),
        P(("space", "blk"), None),
        P(("space", "blk"), None),
        P(("space", "blk"), None),
        P(),
        P(),
    )
    return jax.shard_map(
        shards,
        mesh=mesh,
        in_specs=placed,
        out_specs=(P(("space", "blk"), None, None), P(("space", "blk"), None)),
        check_vma=False,
    )
```

```python
import jax
import jax.numpy as jnp
from jax import lax
from jax.experimental import pallas as pl
from jax.experimental.pallas import tpu as pltpu
from jax.sharding import PartitionSpec as P

def tile_of(blocks, most=48):
    for tile in range(most, 7, -8):
        if blocks % tile == 0:
            return tile
    return blocks


def moments_kernel(dens_ref, bra_ref, ket_ref, out_ref):
    for j in range(out_ref.shape[0]):
        mixed = jnp.dot(dens_ref[j], ket_ref[j], preferred_element_type=jnp.float32)
        out_ref[pl.ds(j, 1), :] = jnp.sum(
            bra_ref[j].astype(jnp.float32) * mixed, axis=0, keepdims=True
        )


def block_moments(density, bra_table, ket_table):
    blocks, rows, cols = density.shape
    coeffs = bra_table.shape[2]
    tile = tile_of(blocks)
    return pl.pallas_call(
        moments_kernel,
        out_shape=jax.ShapeDtypeStruct((blocks, coeffs), jnp.float32),
        grid=(blocks // tile,),
        in_specs=[
            pl.BlockSpec((tile, rows, cols), lambda i: (i, 0, 0)),
            pl.BlockSpec((tile, rows, coeffs), lambda i: (i, 0, 0)),
            pl.BlockSpec((tile, cols, coeffs), lambda i: (i, 0, 0)),
        ],
        out_specs=pl.BlockSpec((tile, coeffs), lambda i: (i, 0)),
        cost_estimate=pl.CostEstimate(
            flops=2 * blocks * rows * cols * coeffs,
            transcendentals=0,
            bytes_accessed=2 * blocks * (rows * cols + 2 * rows * coeffs) + 4 * blocks * coeffs,
        ),
    )(density, bra_table, ket_table)


def coulomb_kernel(ids_ref, bra_ref, ket_ref, local_ref, out_ref):
    tile = out_ref.shape[0]
    first = pl.program_id(0) * tile
    for j in range(tile):
        local = local_ref[pl.ds(ids_ref[first + j], 1), :]
        scaled = (bra_ref[j].astype(jnp.float32) * local).astype(jnp.bfloat16)
        out_ref[j] = lax.dot_general(
            scaled, ket_ref[j], (((1,), (1,)), ((), ())), preferred_element_type=jnp.float32
        ).astype(jnp.bfloat16)


def block_coulomb(bra_table, ket_table, domain_local, box_ids):
    blocks, rows, coeffs = bra_table.shape
    cols = ket_table.shape[1]
    boxes = domain_local.shape[0]
    tile = tile_of(blocks, most=96)
    return pl.pallas_call(
        coulomb_kernel,
        out_shape=jax.ShapeDtypeStruct((blocks, rows, cols), jnp.bfloat16),
        grid_spec=pltpu.PrefetchScalarGridSpec(
            num_scalar_prefetch=1,
            grid=(blocks // tile,),
            in_specs=[
                pl.BlockSpec((tile, rows, coeffs), lambda i, ids: (i, 0, 0)),
                pl.BlockSpec((tile, cols, coeffs), lambda i, ids: (i, 0, 0)),
                pl.BlockSpec((boxes, coeffs), lambda i, ids: (0, 0)),
            ],
            out_specs=pl.BlockSpec((tile, rows, cols), lambda i, ids: (i, 0, 0)),
        ),
        cost_estimate=pl.CostEstimate(
            flops=2 * blocks * rows * cols * coeffs,
            transcendentals=0,
            bytes_accessed=2 * blocks * (rows * cols + 2 * rows * coeffs) + 4 * boxes * coeffs,
        ),
    )(box_ids, bra_table, ket_table, domain_local)


def exchange(x, axis, mask):
    count = lax.axis_size(axis)
    return lax.ppermute(x, axis, [(i, i ^ mask) for i in range(count)])


def butterfly_sum(x, axis):
    count = lax.axis_size(axis)
    mask = 1
    while mask < count:
        x = x + exchange(x, axis, mask)
        mask *= 2
    return x


def butterfly_gather(x, axis):
    count = lax.axis_size(axis)
    me = lax.axis_index(axis)
    mask = 1
    while mask < count:
        other = exchange(x, axis, mask)
        low = (me // mask) % 2 == 0
        x = jnp.where(low, jnp.concatenate([x, other], 0), jnp.concatenate([other, x], 0))
        mask *= 2
    return x


def shards(
    density,
    bra_table,
    ket_table,
    box_of_block,
    leaf_src,
    leaf_type,
    coarse_src,
    coarse_type,
    translation,
    upward_translation_table,
):
    top = lax.Precision.HIGH
    n_blk = lax.axis_size("blk")
    n_space = lax.axis_size("space")
    me = lax.axis_index("blk")
    here = lax.axis_index("space")
    leaves = leaf_src.shape[0]
    box_dom = leaves * n_blk
    n_types = translation.shape[0]
    coeffs = translation.shape[1]

    core = me % 2
    core0 = core == 0
    half = box_dom // 2

    lists = jnp.concatenate([leaf_src, leaf_type, coarse_src, coarse_type], axis=0)
    flat = lists.size
    slot_rows = -(-flat // coeffs)
    slot = jnp.pad(lists.reshape(flat).astype(jnp.float32), (0, slot_rows * coeffs - flat))
    slot = slot.reshape(slot_rows, coeffs)

    moments = block_moments(density, bra_table, ket_table)
    box_hot = (box_of_block[:, None] == jnp.arange(box_dom, dtype=jnp.int32)[None, :]).astype(
        jnp.float32
    )
    partial_moments = lax.dot_general(
        box_hot, moments, (((0,), (0,)), ((), ())), precision=top
    )
    first = partial_moments[:half]
    second = partial_moments[half:]
    got = exchange(jnp.concatenate([jnp.where(core0, second, first), slot], axis=0), "blk", 1)
    summed = jnp.where(core0, first, second) + got[:half]
    gathered_lists = jnp.concatenate([slot, got[half:]], axis=0)
    mask = 2
    while mask < n_blk:
        got = exchange(jnp.concatenate([summed, gathered_lists], axis=0), "blk", mask)
        summed = summed + got[:half]
        gathered_lists = jnp.concatenate([gathered_lists, got[half:]], axis=0)
        mask *= 2
    leaf_half = summed
    base = me - core
    by_slot = gathered_lists.reshape(n_blk, slot_rows * coeffs)
    paired = by_slot.reshape(n_blk // 2, 2, -1)[:, ::-1].reshape(n_blk, -1)
    by_slot = jnp.where(core0, by_slot, paired)

    parent_half = jnp.einsum(
        "qce,cde->qd", leaf_half.reshape(-1, 8, coeffs), upward_translation_table, precision=top
    )
    p_half = parent_half.shape[0]
    parents = parent_half
    carried = leaf_half
    delivered = []
    mask = 1
    while mask < n_space:
        got = exchange(jnp.concatenate([carried, parents], axis=0), "space", mask)
        carried = got[:half]
        delivered.append(carried)
        parents = jnp.concatenate([parents, got[half:]], axis=0)
        mask *= 2

    def neighbour(step):
        other = here + step
        pick = jnp.zeros_like(leaf_half)
        for r, block in enumerate(delivered):
            pick = jnp.where((here ^ other) == 2 ** (r + 1) - 1, block, pick)
        inside = (other >= 0) & (other < n_space)
        return jnp.where(inside, pick, 0.0)

    window = jnp.concatenate([neighbour(-1), leaf_half, neighbour(1)], axis=0)
    rows_held = (
        jnp.arange(3)[:, None] * box_dom + core * half + jnp.arange(half)[None, :]
    ).reshape(-1)
    slots = parents.shape[0] // p_half
    parents_held = (
        jnp.arange(slots)[:, None] * n_blk + core * p_half + jnp.arange(p_half)[None, :]
    ).reshape(-1)
    table = by_slot[:, :flat].reshape((n_blk,) + lists.shape).astype(jnp.int32)
    dom_src = table[:, :leaves].reshape(box_dom, -1)
    dom_type = table[:, leaves : 2 * leaves].reshape(box_dom, -1)
    dom_csrc = table[:, 2 * leaves]
    dom_ctype = table[:, 2 * leaves + 1]
    dom_csrc = (dom_csrc // n_blk ^ here) * n_blk + dom_csrc % n_blk

    src_hot = (dom_src[..., None] == rows_held).astype(jnp.bfloat16)
    type_hot = (dom_type[..., None] == jnp.arange(n_types, dtype=jnp.int32)).astype(jnp.bfloat16)
    counts = jnp.einsum("blt,blj->btj", type_hot, src_hot, preferred_element_type=jnp.float32)
    gathered = jnp.einsum("btj,jk->btk", counts, window, precision=top)
    csrc_hot = (dom_csrc[..., None] == parents_held).astype(jnp.bfloat16)
    ctype_hot = (dom_ctype[..., None] == jnp.arange(n_types, dtype=jnp.int32)).astype(jnp.bfloat16)
    ccounts = jnp.einsum("pet,peq->ptq", ctype_hot, csrc_hot, preferred_element_type=jnp.float32)
    cgathered = jnp.einsum("ptq,qk->ptk", ccounts, parents, precision=top)
    rows = jnp.concatenate([gathered, cgathered], axis=0)
    far_part = jnp.einsum("btk,tlk->bl", rows, translation, precision=top)
    far = far_part + exchange(far_part, "blk", 1)
    leaf_far = far[:box_dom]
    parent_locals = far[box_dom:]
    downward = jnp.einsum(
        "qd,cds->qcs", parent_locals, upward_translation_table, precision=top
    ).reshape(box_dom, coeffs)
    domain_local = leaf_far + downward
    box_locals = lax.dynamic_slice_in_dim(domain_local, core * leaves, leaves, axis=0)
    relabelled = ((box_of_block // leaves) ^ base) * leaves + box_of_block % leaves
    coulomb = block_coulomb(bra_table, ket_table, domain_local, relabelled)
    return (coulomb, box_locals)


def solution(mesh):
    placed = (
        P(("space", "blk"), None, None),
        P(("space", "blk"), None, None),
        P(("space", "blk"), None, None),
        P(("space", "blk")),
        P(("space", "blk"), None),
        P(("space", "blk"), None),
        P(("space", "blk"), None),
        P(("space", "blk"), None),
        P(),
        P(),
    )
    return jax.shard_map(
        shards,
        mesh=mesh,
        in_specs=placed,
        out_specs=(P(("space", "blk"), None, None), P(("space", "blk"), None)),
        check_vma=False,
    )
```
